128 devices in a mesh: enc: 16 (over z, y), dp: 2 (over x_hi), tensor: 4 (over x_lo, core).
Axes of the slice: x: 4 (x_hi: 2, x_lo: 2; x = x_hi * 2 + x_lo), y: 4, z: 4, core: 2. Of those that a mesh axis runs over, the one named last changes fastest.
Arguments:
- hidden_in: bfloat16 [3, 64, 4096], P(None, 'dp', 'enc')
- self_cache: bfloat16 [64, 8, 2, 2048], P(('dp', 'enc'), None, None, 'tensor'), may hold values from -6 to 6
- src_pool: bfloat16 [64, 24, 2, 2048], P(('dp', 'enc'), None, None, 'tensor'), may hold values from -6 to 6
- assign: int32 [64], replicated, may hold values from 0 to 63, as said below
- src_len: int32 [64], replicated, may hold values from 1 to 24, 768 in all
- positions: int32 [64], replicated, may hold values from 1 to 8, 256 in all
- gain_self: float32 [4096], P('enc'), may hold values from 0.1 to 1.9
- w_qkv: bfloat16 [4096, 3, 2048], P('enc', None, 'tensor'), may hold values from -0.09375 to 0.09375
- w_out_self: bfloat16 [2048, 4096], P('tensor', 'enc'), may hold values from -0.125 to 0.125
- gain_cross: float32 [4096], P('enc'), may hold values from 0.1 to 1.9
- w_q_cross: bfloat16 [4096, 2048], P('enc', 'tensor'), may hold values from -0.09375 to 0.09375
- w_out_cross: bfloat16 [2048, 4096], P('tensor', 'enc'), may hold values from -0.125 to 0.125
Outputs:
- layer_out: bfloat16 [3, 64, 4096], P(None, 'dp', 'enc')
The draws below stay inside these ranges and needn't reach their ends.
Inputs may be any that keep to these rules, and one draw needn't show every extreme that they name: `assign`: a permutation of the 64 sources; with blocks of 2 consecutive sequences or sources numbered d * 16 + e, the 2 sequences of block d * 16 + e read exactly one source from each block d2 * 16 + e that has the same e.
All inputs are finite; a program needn't handle non-finite values.
Results may differ from the reference program's by a relative error of at most 0.008.
Values may be sent and summed in bfloat16 or wider, within the bound.
No kernel may reach another device: no remote copies, remote signals or barrier semaphores. Data moves between devices by JAX's collectives and lax.ppermute only.
A program may use at most 64 MiB of HBM per device.

```python
import math
import jax
import jax.numpy as jnp
import numpy as np
from jax import lax

D = 4096
HEADS = 8
DK = 256
STEPS = 3
SRC = 24
PMAX = 8
INNER = 2048
SEQ_DEV = 2
NSEQ = 64
NSRC = 64
N_ENC = 16
N_DP = 2


def draw_hidden_in(key, part):
    key_normal, key_column, key_row = jax.random.split(key, 3)
    column_at = jnp.arange(D, dtype=jnp.float32) / D
    column_rand = jax.random.uniform(key_column, (D,), jnp.float32)
    row_rand = jax.random.uniform(key_row, (STEPS, NSEQ, 1), jnp.float32)
    values = jax.random.normal(key_normal, (STEPS, NSEQ, D), jnp.float32)
    column_scale = 0.3 * 10.0 ** (0.5 * column_at + 0.5 * column_rand)
    row_scale = 0.5 * 4.0 ** row_rand
    return (values * column_scale[None, None, :] * row_scale).astype(jnp.bfloat16)


def assign_within(key_send, key_local):
    block_count = N_DP
    base_list = jnp.arange(SEQ_DEV, dtype=jnp.int32) % block_count
    senders = jax.vmap(lambda one_key: jax.random.permutation(one_key, base_list))(jax.random.split(key_send, block_count))
    flat_send = senders.reshape(-1)
    flat_index = jnp.arange(block_count * SEQ_DEV, dtype=jnp.int32)
    earlier = (flat_send[None, :] == flat_send[:, None]) & (flat_index[None, :] < flat_index[:, None])
    slot_rank = jnp.sum(earlier.astype(jnp.int32), axis=1).astype(jnp.int32)
    local_perm = jax.vmap(lambda one_key: jax.random.permutation(one_key, SEQ_DEV))(jax.random.split(key_local, block_count)).astype(jnp.int32)
    return (flat_send.astype(jnp.int32), local_perm[flat_send, slot_rank].astype(jnp.int32))


def draw_assign(key, part):
    key_send, key_local = jax.random.split(key)
    sender_block, sender_row = jax.vmap(assign_within)(jax.random.split(key_send, N_ENC), jax.random.split(key_local, N_ENC))
    enc_column = jnp.arange(N_ENC, dtype=jnp.int32)[:, None]
    global_source = (sender_block * N_ENC + enc_column) * SEQ_DEV + sender_row
    arranged = jnp.transpose(global_source.reshape(N_ENC, N_DP, SEQ_DEV), (1, 0, 2))
    return arranged.reshape(-1).astype(jnp.int32)


def block_scale(stream_key, extent, cuts, smallest, largest):
    def one(axis_at, parts):
        steps = jax.random.uniform(jax.random.fold_in(jax.random.fold_in(stream_key, 6), axis_at), (parts,), jnp.float32, smallest / len(cuts), largest / len(cuts))
        return jnp.repeat(jnp.exp(steps), extent[axis_at] // parts).reshape((-1,) + (1,) * (len(extent) - axis_at - 1))

    factor_of = one(*cuts[0])
    for cut in cuts[1:]:
        factor_of = factor_of * one(*cut)
    return factor_of


def split_up(number_of, total, reach, slope):
    weights = [(1 << 20) // math.isqrt(grade ** slope) + 1 for grade in range(2, number_of + 1)]
    spare, counts = total - reach - (number_of - 1), [1] * (number_of - 1)
    while spare > 0:
        free = [i for i in range(number_of - 1) if counts[i] < reach]
        mass, budget = sum([weights[i] for i in free]), spare
        for i in free:
            extra = min(reach - counts[i], max(1, budget * weights[i] // mass), spare)
            counts[i] = counts[i] + extra
            spare = spare - extra
    return np.array([reach] + counts)


def uneven(rng, number_of, total, most, skew):
    if number_of == 2:
        one = jax.random.randint(rng, (), max(1, total - most), min(most, total - 1) + 1)
        return jnp.stack([one, total - one])
    lengths = jnp.asarray(split_up(number_of, total, most, skew), jnp.int32)
    pairs = (number_of - 1) // 2
    giver, sink = lengths[1:1 + 2 * pairs:2], lengths[2:2 + 2 * pairs:2]
    room = jnp.minimum(giver - 1, most - sink)
    moved = jax.random.randint(jax.random.fold_in(rng, 1), (pairs,), 0, 1 << 20) % (room + 1)
    lengths = lengths.at[1:1 + 2 * pairs:2].set(giver - moved).at[2:2 + 2 * pairs:2].set(sink + moved)
    return lengths[jax.random.permutation(jax.random.fold_in(rng, 2), number_of)]


def centred(stream_key, extent, width, bound, cuts=(), kind=jnp.bfloat16):
    level = block_scale(stream_key, extent, cuts, -0.22, 0.18) if cuts else 1.0
    array = jax.random.normal(stream_key, extent, jnp.float32) * width * level
    return jnp.minimum(jnp.maximum(array, -bound), bound).astype(kind)


def setup_inputs(seed: int = 0) -> dict:
    arg_keys = jax.random.split(jax.random.key(seed), 13)
    hidden_in = draw_hidden_in(jax.random.fold_in(arg_keys[12], 71), 0)
    self_cache = centred(arg_keys[1], (NSEQ, PMAX, 2, INNER), 1.0, 6.0, ((0, 32), (3, 4)))
    src_pool = centred(arg_keys[2], (NSRC, SRC, 2, INNER), 1.0, 6.0, ((0, 32), (3, 4)))
    assign = draw_assign(jax.random.fold_in(arg_keys[12], 71), 0)
    src_len = uneven(arg_keys[4], NSRC, NSRC * SRC // 2, SRC, 2).astype(jnp.int32)
    positions = uneven(arg_keys[5], NSEQ, NSEQ * PMAX // 2, PMAX, 2).astype(jnp.int32)
    gain_self = jnp.clip(1.0 + 0.18 * jax.random.normal(arg_keys[6], (D,), jnp.float32), 0.1, 1.9)
    w_qkv = centred(arg_keys[7], (D, 3, INNER), D ** -0.5, 0.09375, ((0, 16), (2, 4)))
    w_out_self = centred(arg_keys[8], (INNER, D), INNER ** -0.5, 0.125, ((0, 4), (1, 16)))
    gain_cross = jnp.clip(1.0 + 0.18 * jax.random.normal(arg_keys[9], (D,), jnp.float32), 0.1, 1.9)
    w_q_cross = centred(arg_keys[10], (D, INNER), D ** -0.5, 0.09375, ((0, 16), (1, 4)))
    w_out_cross = centred(arg_keys[11], (INNER, D), INNER ** -0.5, 0.125, ((0, 4), (1, 16)))
    return {"hidden_in": hidden_in, "self_cache": self_cache, "src_pool": src_pool, "assign": assign, "src_len": src_len, "positions": positions, "gain_self": gain_self, "w_qkv": w_qkv, "w_out_self": w_out_self, "gain_cross": gain_cross, "w_q_cross": w_q_cross, "w_out_cross": w_out_cross}


EPSILON = 1e-06

def row_norm(rows_in, gain_vec):
    squares = lax.optimization_barrier(jnp.sum(rows_in * rows_in, axis=1)) / D
    return (rows_in * lax.rsqrt(squares + EPSILON)[:, None] * gain_vec[None, :]).astype(jnp.bfloat16)

def score_weight(scores):
    rounded = jnp.exp(scores).astype(jnp.bfloat16)
    return lax.optimization_barrier(rounded).astype(jnp.float32)

def attend_one(pieces):
    query_row, key_block, value_block, usable = pieces
    query_heads = query_row.astype(jnp.float32).reshape(HEADS, DK)
    key_heads = key_block.astype(jnp.float32).reshape(-1, HEADS, DK)
    value_heads = value_block.astype(jnp.float32).reshape(-1, HEADS, DK)
    scores = jnp.einsum('hd,lhd->hl', query_heads, key_heads) * (1.0 / math.sqrt(DK))
    weights = jnp.where(usable[None, :], score_weight(scores), 0.0)
    weighted = jnp.einsum('hl,lhd->hd', weights, value_heads)
    return (weighted, lax.optimization_barrier(jnp.sum(weights, axis=-1)))

def reference(hidden_in, self_cache, src_pool, assign, src_len, positions, gain_self, w_qkv, w_out_self, gain_cross, w_q_cross, w_out_cross):
    place_index = jnp.arange(PMAX, dtype=jnp.int32)
    cache_usable = place_index[None, :] < positions[:, None]
    token_index = jnp.arange(SRC, dtype=jnp.int32)
    cross_len = jnp.take(src_len, assign)
    cross_usable = token_index[None, :] < cross_len[:, None]
    weight_qkv = w_qkv.reshape(D, 3 * INNER)

    def cross_one(pieces):
        query_row, source_id, usable = pieces
        block = src_pool[source_id]
        return attend_one((query_row, block[:, 0], block[:, 1], usable))
    results = []
    key_list = []
    value_list = []
    for step_at in range(STEPS):
        current = hidden_in[step_at].astype(jnp.float32)
        normed = row_norm(current, gain_self)
        projected = jnp.dot(normed, weight_qkv, preferred_element_type=jnp.float32).reshape(NSEQ, 3, INNER).astype(jnp.bfloat16)
        query_rows = projected[:, 0]
        key_list.append(projected[:, 1])
        value_list.append(projected[:, 2])
        weighted, totals = lax.map(attend_one, (query_rows, self_cache[:, :, 0], self_cache[:, :, 1], cache_usable))
        query_heads = query_rows.astype(jnp.float32).reshape(NSEQ, HEADS, DK)
        for key_new, value_new in zip(key_list, value_list):
            scores = lax.optimization_barrier(jnp.sum(query_heads * key_new.astype(jnp.float32).reshape(NSEQ, HEADS, DK), axis=-1)) * (1.0 / math.sqrt(DK))
            weights = score_weight(scores)
            weighted = weighted + weights[:, :, None] * value_new.astype(jnp.float32).reshape(NSEQ, HEADS, DK)
            totals = totals + weights
        context = (weighted / totals[:, :, None]).reshape(NSEQ, INNER).astype(jnp.bfloat16)
        residual = current + jnp.dot(context, w_out_self, preferred_element_type=jnp.float32)
        normed_cross = row_norm(residual, gain_cross)
        cross_query = jnp.dot(normed_cross, w_q_cross, preferred_element_type=jnp.float32).astype(jnp.bfloat16)
        weighted, totals = lax.map(cross_one, (cross_query, assign, cross_usable))
        context = (weighted / totals[:, :, None]).reshape(NSEQ, INNER).astype(jnp.bfloat16)
        output_rows = residual + jnp.dot(context, w_out_cross, preferred_element_type=jnp.float32)
        results.append(output_rows.astype(jnp.bfloat16))
    return jnp.stack(results)
```

```python
import math

import jax
import jax.numpy as jnp
from jax import lax
from jax.sharding import PartitionSpec as P

D = 4096
DK = 256


EPSILON = 1e-06
LANE = 128


def score_weight(scores):
    return jnp.exp(scores).astype(jnp.bfloat16)


def rows_reduce_scatter(partial, owned):
    n_enc = lax.axis_size("enc")
    steps, rows, cols = partial.shape
    send = partial.reshape(steps, n_enc, owned, cols).transpose(1, 0, 2, 3)
    got = lax.all_to_all(send, "enc", 0, 0, tiled=True)
    return jnp.sum(got, axis=0)


def rows_gather(chunk):
    n_enc = lax.axis_size("enc")
    steps, owned, width = chunk.shape
    send = jnp.broadcast_to(chunk[None], (n_enc, steps, owned, width))
    got = lax.all_to_all(send, "enc", 0, 0, tiled=True)
    return got.transpose(1, 0, 2, 3).reshape(steps, n_enc * owned, width)


def tensor_sum(value):
    n_t = lax.axis_size("tensor")
    bit = 1
    while bit < n_t:
        other = lax.ppermute(value, "tensor", [(i, i ^ bit) for i in range(n_t)])
        value = value + other
        bit *= 2
    return value


def with_sumsq(partial, rows_in):
    squares = jnp.sum(rows_in * rows_in, axis=-1, keepdims=True)
    pad = jnp.zeros(rows_in.shape[:-1] + (LANE - 1,), jnp.float32)
    return jnp.concatenate([partial, squares, pad], axis=-1)


def split_norm(packed, width):
    scale = lax.rsqrt(packed[..., width] / D + EPSILON)
    return (packed[..., :width] * scale[..., None]).astype(jnp.bfloat16)


def on_device(
    hidden_in,
    self_cache,
    src_pool,
    assign,
    src_len,
    positions,
    gain_self,
    w_qkv,
    w_out_self,
    gain_cross,
    w_q_cross,
    w_out_cross,
):
    dp_count = lax.axis_size("dp")
    enc_count = lax.axis_size("enc")
    seq_dev = self_cache.shape[0]
    per_pair = seq_dev // dp_count
    cache_len = self_cache.shape[1]
    source_len = src_pool.shape[1]
    width = self_cache.shape[3]
    head_count = width // DK
    steps = hidden_in.shape[0]
    enc_at = lax.axis_index("enc")
    dp_at = lax.axis_index("dp")
    block_at = dp_at * enc_count + enc_at
    slot_index = jnp.arange(seq_dev, dtype=jnp.int32)
    my_slots = block_at * seq_dev + slot_index
    my_positions = jnp.take(positions, my_slots)
    my_sources = jnp.take(assign, my_slots)
    place_at = jnp.arange(cache_len, dtype=jnp.int32)
    cache_usable = place_at[None, :] < my_positions[:, None]
    token_at = jnp.arange(source_len, dtype=jnp.int32)
    assign_view = assign.reshape(dp_count, enc_count, seq_dev)
    assign_grid = jnp.take(assign_view, enc_at, axis=1)
    owners = assign_grid // (seq_dev * enc_count)
    earlier = (owners[:, None, :] == owners[:, :, None]) & (
        slot_index[None, None, :] < slot_index[None, :, None]
    )
    slot_rank = jnp.sum(earlier.astype(jnp.int32), axis=2)
    recv_rows = jnp.take(owners, dp_at, axis=0) * per_pair + jnp.take(slot_rank, dp_at, axis=0)
    picked = (owners == dp_at)[:, :, None] & (
        slot_rank[:, :, None] == jnp.arange(per_pair, dtype=jnp.int32)[None, None, :]
    )
    chosen = jnp.sum(jnp.where(picked, (assign_grid % seq_dev)[:, :, None], 0), axis=1)
    chosen_flat = chosen.reshape(-1)
    outgoing = jnp.take(src_pool, chosen_flat, axis=0)
    arrived = lax.all_to_all(outgoing, "dp", split_axis=0, concat_axis=0, tiled=True)
    cross_kv = jnp.take(arrived, recv_rows, axis=0)
    cross_usable = token_at[None, :] < jnp.take(src_len, my_sources)[:, None]

    current = hidden_in.astype(jnp.float32)
    scaled = (current * gain_self[None, None, :]).astype(jnp.bfloat16)
    proj = jnp.einsum("tsd,dcw->tscw", scaled, w_qkv, preferred_element_type=jnp.float32)
    proj = proj.reshape(steps, current.shape[1], 3 * width)
    own = rows_reduce_scatter(with_sumsq(proj, current), seq_dev)
    qkv = split_norm(own, 3 * width).reshape(steps, seq_dev, 3, head_count, DK)
    query = qkv[:, :, 0]
    key_new = qkv[:, :, 1]
    value_new = qkv[:, :, 2]

    inv = 1.0 / math.sqrt(DK)
    cache_keys = self_cache[:, :, 0].reshape(seq_dev, cache_len, head_count, DK)
    cache_values = self_cache[:, :, 1].reshape(seq_dev, cache_len, head_count, DK)
    s_cache = jnp.einsum(
        "tnhd,nlhd->tnhl", query, cache_keys, preferred_element_type=jnp.float32
    ) * inv
    w_cache = jnp.where(
        cache_usable[None, :, None, :], score_weight(s_cache), jnp.zeros((), jnp.bfloat16)
    )
    s_new = jnp.einsum(
        "tnhd,unhd->tnhu", query, key_new, preferred_element_type=jnp.float32
    ) * inv
    step_at = jnp.arange(steps, dtype=jnp.int32)
    new_usable = step_at[None, :] <= step_at[:, None]
    w_new = jnp.where(
        new_usable[:, None, None, :], score_weight(s_new), jnp.zeros((), jnp.bfloat16)
    )
    weighted = jnp.einsum(
        "tnhl,nlhd->tnhd", w_cache, cache_values, preferred_element_type=jnp.float32
    ) + jnp.einsum("tnhu,unhd->tnhd", w_new, value_new, preferred_element_type=jnp.float32)
    totals = jnp.sum(w_cache.astype(jnp.float32), axis=-1) + jnp.sum(
        w_new.astype(jnp.float32), axis=-1
    )
    context = (weighted / totals[..., None]).reshape(steps, seq_dev, width).astype(jnp.bfloat16)
    context_all = rows_gather(context)
    residual = current + tensor_sum(
        jnp.einsum("tsw,wf->tsf", context_all, w_out_self, preferred_element_type=jnp.float32)
    )

    scaled = (residual * gain_cross[None, None, :]).astype(jnp.bfloat16)
    cq = jnp.einsum("tsd,dw->tsw", scaled, w_q_cross, preferred_element_type=jnp.float32)
    own = rows_reduce_scatter(with_sumsq(cq, residual), seq_dev)
    cross_query = split_norm(own, width).reshape(steps, seq_dev, head_count, DK)
    cross_keys = cross_kv[:, :, 0].reshape(seq_dev, source_len, head_count, DK)
    cross_values = cross_kv[:, :, 1].reshape(seq_dev, source_len, head_count, DK)
    s_cross = jnp.einsum(
        "tnhd,nlhd->tnhl", cross_query, cross_keys, preferred_element_type=jnp.float32
    ) * inv
    w_cross = jnp.where(
        cross_usable[None, :, None, :], score_weight(s_cross), jnp.zeros((), jnp.bfloat16)
    )
    weighted = jnp.einsum(
        "tnhl,nlhd->tnhd", w_cross, cross_values, preferred_element_type=jnp.float32
    )
    totals = jnp.sum(w_cross.astype(jnp.float32), axis=-1)
    context = (weighted / totals[..., None]).reshape(steps, seq_dev, width).astype(jnp.bfloat16)
    context_all = rows_gather(context)
    output_rows = residual + tensor_sum(
        jnp.einsum("tsw,wf->tsf", context_all, w_out_cross, preferred_element_type=jnp.float32)
    )
    return output_rows.astype(jnp.bfloat16)


def solution(mesh):
    in_specs = (
        P(None, "dp", "enc"),
        P(("dp", "enc"), None, None, "tensor"),
        P(("dp", "enc"), None, None, "tensor"),
        P(),
        P(),
        P(),
        P("enc"),
        P("enc", None, "tensor"),
        P("tensor", "enc"),
        P("enc"),
        P("enc", "tensor"),
        P("tensor", "enc"),
    )
    out_specs = P(None, "dp", "enc")
    return jax.shard_map(
        on_device, mesh=mesh, in_specs=in_specs, out_specs=out_specs, check_vma=False
    )
```

```python
import math

import jax
import jax.numpy as jnp
from jax import lax
from jax.sharding import PartitionSpec as P

D = 4096
DK = 256


EPSILON = 1e-06
LANE = 128


def score_weight(scores):
    return jnp.exp(scores).astype(jnp.bfloat16)


def rows_gather(chunk):
    n_enc = lax.axis_size("enc")
    steps, owned, width = chunk.shape
    send = jnp.broadcast_to(chunk[None], (n_enc, steps, owned, width))
    got = lax.all_to_all(send, "enc", 0, 0, tiled=True)
    return got.transpose(1, 0, 2, 3).reshape(steps, n_enc * owned, width)


def tensor_sum(value):
    n_t = lax.axis_size("tensor")
    bit = 1
    while bit < n_t:
        other = lax.ppermute(value, "tensor", [(i, i ^ bit) for i in range(n_t)])
        value = value + other
        bit *= 2
    return value


def with_sumsq(partial, rows_in):
    squares = jnp.sum(rows_in * rows_in, axis=-1, keepdims=True)
    high = squares.astype(jnp.bfloat16)
    low = (squares - high.astype(jnp.float32)).astype(jnp.bfloat16)
    pad = jnp.zeros(rows_in.shape[:-1] + (LANE - 2,), jnp.bfloat16)
    return jnp.concatenate([partial.astype(jnp.bfloat16), high, low, pad], axis=-1)


def rows_reduce_scatter(partial, owned):
    n_enc = lax.axis_size("enc")
    steps, rows, cols = partial.shape
    send = partial.reshape(steps, n_enc, owned, cols).transpose(1, 0, 2, 3)
    got = lax.all_to_all(send, "enc", 0, 0, tiled=True)
    return jnp.sum(got.astype(jnp.float32), axis=0)


def split_norm(packed, width):
    squares = packed[..., width] + packed[..., width + 1]
    scale = lax.rsqrt(squares / D + EPSILON)
    return (packed[..., :width] * scale[..., None]).astype(jnp.bfloat16)


def on_device(
    hidden_in,
    self_cache,
    src_pool,
    assign,
    src_len,
    positions,
    gain_self,
    w_qkv,
    w_out_self,
    gain_cross,
    w_q_cross,
    w_out_cross,
):
    dp_count = lax.axis_size("dp")
    enc_count = lax.axis_size("enc")
    seq_dev = self_cache.shape[0]
    per_pair = seq_dev // dp_count
    cache_len = self_cache.shape[1]
    source_len = src_pool.shape[1]
    width = self_cache.shape[3]
    head_count = width // DK
    steps = hidden_in.shape[0]
    enc_at = lax.axis_index("enc")
    dp_at = lax.axis_index("dp")
    block_at = dp_at * enc_count + enc_at
    slot_index = jnp.arange(seq_dev, dtype=jnp.int32)
    my_slots = block_at * seq_dev + slot_index
    my_positions = jnp.take(positions, my_slots)
    my_sources = jnp.take(assign, my_slots)
    place_at = jnp.arange(cache_len, dtype=jnp.int32)
    cache_usable = place_at[None, :] < my_positions[:, None]
    token_at = jnp.arange(source_len, dtype=jnp.int32)
    assign_view = assign.reshape(dp_count, enc_count, seq_dev)
    assign_grid = jnp.take(assign_view, enc_at, axis=1)
    owners = assign_grid // (seq_dev * enc_count)
    earlier = (owners[:, None, :] == owners[:, :, None]) & (
        slot_index[None, None, :] < slot_index[None, :, None]
    )
    slot_rank = jnp.sum(earlier.astype(jnp.int32), axis=2)
    recv_rows = jnp.take(owners, dp_at, axis=0) * per_pair + jnp.take(slot_rank, dp_at, axis=0)
    picked = (owners == dp_at)[:, :, None] & (
        slot_rank[:, :, None] == jnp.arange(per_pair, dtype=jnp.int32)[None, None, :]
    )
    chosen = jnp.sum(jnp.where(picked, (assign_grid % seq_dev)[:, :, None], 0), axis=1)
    chosen_flat = chosen.reshape(-1)
    outgoing = jnp.take(src_pool, chosen_flat, axis=0).reshape(
        (dp_count, per_pair) + src_pool.shape[1:]
    )
    pieces = []
    for shift in range(dp_count):
        if shift == 0:
            pieces.append(jnp.take(outgoing, dp_at, axis=0))
        else:
            sent = jnp.take(outgoing, (dp_at + shift) % dp_count, axis=0)
            pieces.append(
                lax.ppermute(
                    sent, "dp", [(i, (i + shift) % dp_count) for i in range(dp_count)]
                )
            )
    stacked = jnp.stack(pieces)
    sender_at = (dp_at - jnp.arange(dp_count, dtype=jnp.int32)) % dp_count
    order = jnp.argsort(sender_at)
    arrived = jnp.take(stacked, order, axis=0).reshape((seq_dev,) + src_pool.shape[1:])
    cross_kv = jnp.take(arrived, recv_rows, axis=0)
    cross_usable = token_at[None, :] < jnp.take(src_len, my_sources)[:, None]

    current = hidden_in.astype(jnp.float32)
    scaled = (current * gain_self[None, None, :]).astype(jnp.bfloat16)
    proj = jnp.einsum("tsd,dcw->tscw", scaled, w_qkv, preferred_element_type=jnp.float32)
    proj = proj.reshape(steps, current.shape[1], 3 * width)
    own = rows_reduce_scatter(with_sumsq(proj, current), seq_dev)
    qkv = split_norm(own, 3 * width).reshape(steps, seq_dev, 3, head_count, DK)
    query = qkv[:, :, 0]
    key_new = qkv[:, :, 1]
    value_new = qkv[:, :, 2]

    inv = 1.0 / math.sqrt(DK)
    cache_keys = self_cache[:, :, 0].reshape(seq_dev, cache_len, head_count, DK)
    cache_values = self_cache[:, :, 1].reshape(seq_dev, cache_len, head_count, DK)
    s_cache = jnp.einsum(
        "tnhd,nlhd->tnhl", query, cache_keys, preferred_element_type=jnp.float32
    ) * inv
    w_cache = jnp.where(
        cache_usable[None, :, None, :], score_weight(s_cache), jnp.zeros((), jnp.bfloat16)
    )
    s_new = jnp.einsum(
        "tnhd,unhd->tnhu", query, key_new, preferred_element_type=jnp.float32
    ) * inv
    step_at = jnp.arange(steps, dtype=jnp.int32)
    new_usable = step_at[None, :] <= step_at[:, None]
    w_new = jnp.where(
        new_usable[:, None, None, :], score_weight(s_new), jnp.zeros((), jnp.bfloat16)
    )
    weighted = jnp.einsum(
        "tnhl,nlhd->tnhd", w_cache, cache_values, preferred_element_type=jnp.float32
    ) + jnp.einsum("tnhu,unhd->tnhd", w_new, value_new, preferred_element_type=jnp.float32)
    totals = jnp.sum(w_cache.astype(jnp.float32), axis=-1) + jnp.sum(
        w_new.astype(jnp.float32), axis=-1
    )
    context = (weighted / totals[..., None]).reshape(steps, seq_dev, width).astype(jnp.bfloat16)
    context_all = rows_gather(context)
    residual = current + tensor_sum(
        jnp.einsum("tsw,wf->tsf", context_all, w_out_self, preferred_element_type=jnp.float32)
    )

    scaled = (residual * gain_cross[None, None, :]).astype(jnp.bfloat16)
    cq = jnp.einsum("tsd,dw->tsw", scaled, w_q_cross, preferred_element_type=jnp.float32)
    own = rows_reduce_scatter(with_sumsq(cq, residual), seq_dev)
    cross_query = split_norm(own, width).reshape(steps, seq_dev, head_count, DK)
    cross_keys = cross_kv[:, :, 0].reshape(seq_dev, source_len, head_count, DK)
    cross_values = cross_kv[:, :, 1].reshape(seq_dev, source_len, head_count, DK)
    s_cross = jnp.einsum(
        "tnhd,nlhd->tnhl", cross_query, cross_keys, preferred_element_type=jnp.float32
    ) * inv
    w_cross = jnp.where(
        cross_usable[None, :, None, :], score_weight(s_cross), jnp.zeros((), jnp.bfloat16)
    )
    weighted = jnp.einsum(
        "tnhl,nlhd->tnhd", w_cross, cross_values, preferred_element_type=jnp.float32
    )
    totals = jnp.sum(w_cross.astype(jnp.float32), axis=-1)
    context = (weighted / totals[..., None]).reshape(steps, seq_dev, width).astype(jnp.bfloat16)
    context_all = rows_gather(context)
    output_rows = residual + tensor_sum(
        jnp.einsum("tsw,wf->tsf", context_all, w_out_cross, preferred_element_type=jnp.float32)
    )
    return output_rows.astype(jnp.bfloat16)


def solution(mesh):
    in_specs = (
        P(None, "dp", "enc"),
        P(("dp", "enc"), None, None, "tensor"),
        P(("dp", "enc"), None, None, "tensor"),
        P(),
        P(),
        P(),
        P("enc"),
        P("enc", None, "tensor"),
        P("tensor", "enc"),
        P("enc"),
        P("enc", "tensor"),
        P("tensor", "enc"),
    )
    out_specs = P(None, "dp", "enc")
    return jax.shard_map(
        on_device, mesh=mesh, in_specs=in_specs, out_specs=out_specs, check_vma=False
    )
```

```python
import math

import jax
import jax.numpy as jnp
from jax import lax
from jax.sharding import PartitionSpec as P

D = 4096
DK = 256


EPSILON = 1e-06
LANE = 128


def score_weight(scores):
    return jnp.exp(scores).astype(jnp.bfloat16)


def rows_gather(chunk):
    n_enc = lax.axis_size("enc")
    steps, owned, width = chunk.shape
    send = jnp.broadcast_to(chunk[None], (n_enc, steps, owned, width))
    got = lax.all_to_all(send, "enc", 0, 0, tiled=True)
    return got.transpose(1, 0, 2, 3).reshape(steps, n_enc * owned, width)


def tensor_sum(value):
    n_t = lax.axis_size("tensor")
    terms = [value] + [
        lax.ppermute(value, "tensor", [(i, i ^ k) for i in range(n_t)]) for k in range(1, n_t)
    ]
    while len(terms) > 1:
        terms = [terms[k] + terms[k + 1] for k in range(0, len(terms), 2)]
    return terms[0]


def with_sumsq(partial, rows_in):
    squares = jnp.sum(rows_in * rows_in, axis=-1, keepdims=True)
    high = squares.astype(jnp.bfloat16)
    low = (squares - high.astype(jnp.float32)).astype(jnp.bfloat16)
    pad = jnp.zeros(rows_in.shape[:-1] + (LANE - 2,), jnp.bfloat16)
    return jnp.concatenate([partial.astype(jnp.bfloat16), high, low, pad], axis=-1)


def rows_reduce_scatter(partial, owned):
    n_enc = lax.axis_size("enc")
    steps, rows, cols = partial.shape
    send = partial.reshape(steps, n_enc, owned, cols).transpose(1, 0, 2, 3)
    got = lax.all_to_all(send, "enc", 0, 0, tiled=True)
    return jnp.sum(got.astype(jnp.float32), axis=0)


def split_norm(packed, width):
    squares = packed[..., width] + packed[..., width + 1]
    scale = lax.rsqrt(squares / D + EPSILON)
    return (packed[..., :width] * scale[..., None]).astype(jnp.bfloat16)


def on_device(
    hidden_in,
    self_cache,
    src_pool,
    assign,
    src_len,
    positions,
    gain_self,
    w_qkv,
    w_out_self,
    gain_cross,
    w_q_cross,
    w_out_cross,
):
    dp_count = lax.axis_size("dp")
    enc_count = lax.axis_size("enc")
    seq_dev = self_cache.shape[0]
    per_pair = seq_dev // dp_count
    cache_len = self_cache.shape[1]
    source_len = src_pool.shape[1]
    width = self_cache.shape[3]
    head_count = width // DK
    steps = hidden_in.shape[0]
    enc_at = lax.axis_index("enc")
    dp_at = lax.axis_index("dp")
    block_at = dp_at * enc_count + enc_at
    slot_index = jnp.arange(seq_dev, dtype=jnp.int32)
    my_slots = block_at * seq_dev + slot_index
    my_positions = jnp.take(positions, my_slots)
    my_sources = jnp.take(assign, my_slots)
    place_at = jnp.arange(cache_len, dtype=jnp.int32)
    cache_usable = place_at[None, :] < my_positions[:, None]
    token_at = jnp.arange(source_len, dtype=jnp.int32)
    assert seq_dev == dp_count
    my_block = block_at
    source_block = my_sources // seq_dev
    source_row = my_sources % seq_dev
    received = []
    for shift in range(dp_count):
        if shift == 0:
            wanted = my_sources
        else:
            target = (dp_at + shift) % dp_count
            target_slots = (target * enc_count + enc_at) * seq_dev + slot_index
            wanted = jnp.take(assign, target_slots)
        hit = (wanted // seq_dev) == my_block
        row = jnp.sum(jnp.where(hit, wanted % seq_dev, 0))
        piece = lax.dynamic_index_in_dim(src_pool, row, axis=0, keepdims=False)
        if shift:
            piece = lax.ppermute(
                piece, "dp", [(i, (i + shift) % dp_count) for i in range(dp_count)]
            )
        received.append(piece)
    sender_block = [
        ((dp_at - shift) % dp_count) * enc_count + enc_at for shift in range(dp_count)
    ]
    cross_kv = received[0][None]
    cross_kv = jnp.broadcast_to(cross_kv, (seq_dev,) + cross_kv.shape[1:])
    for shift in range(1, dp_count):
        cross_kv = jnp.where(
            (source_block == sender_block[shift])[:, None, None, None],
            received[shift][None],
            cross_kv,
        )
    del source_row
    cross_usable = token_at[None, :] < jnp.take(src_len, my_sources)[:, None]

    current = hidden_in.astype(jnp.float32)
    scaled = (current * gain_self[None, None, :]).astype(jnp.bfloat16)
    proj = jnp.einsum("tsd,dcw->tscw", scaled, w_qkv, preferred_element_type=jnp.float32)
    proj = proj.reshape(steps, current.shape[1], 3 * width)
    own = rows_reduce_scatter(with_sumsq(proj, current), seq_dev)
    qkv = split_norm(own, 3 * width).reshape(steps, seq_dev, 3, head_count, DK)
    query = qkv[:, :, 0]
    key_new = qkv[:, :, 1]
    value_new = qkv[:, :, 2]

    inv = 1.0 / math.sqrt(DK)
    cache_keys = self_cache[:, :, 0].reshape(seq_dev, cache_len, head_count, DK)
    cache_values = self_cache[:, :, 1].reshape(seq_dev, cache_len, head_count, DK)
    s_cache = jnp.einsum(
        "tnhd,nlhd->tnhl", query, cache_keys, preferred_element_type=jnp.float32
    ) * inv
    w_cache = jnp.where(
        cache_usable[None, :, None, :], score_weight(s_cache), jnp.zeros((), jnp.bfloat16)
    )
    s_new = jnp.einsum(
        "tnhd,unhd->tnhu", query, key_new, preferred_element_type=jnp.float32
    ) * inv
    step_at = jnp.arange(steps, dtype=jnp.int32)
    new_usable = step_at[None, :] <= step_at[:, None]
    w_new = jnp.where(
        new_usable[:, None, None, :], score_weight(s_new), jnp.zeros((), jnp.bfloat16)
    )
    weighted = jnp.einsum(
        "tnhl,nlhd->tnhd", w_cache, cache_values, preferred_element_type=jnp.float32
    ) + jnp.einsum("tnhu,unhd->tnhd", w_new, value_new, preferred_element_type=jnp.float32)
    totals = jnp.sum(w_cache.astype(jnp.float32), axis=-1) + jnp.sum(
        w_new.astype(jnp.float32), axis=-1
    )
    context = (weighted / totals[..., None]).reshape(steps, seq_dev, width).astype(jnp.bfloat16)
    context_all = rows_gather(context)
    residual = current + tensor_sum(
        jnp.einsum("tsw,wf->tsf", context_all, w_out_self, preferred_element_type=jnp.float32)
    )

    scaled = (residual * gain_cross[None, None, :]).astype(jnp.bfloat16)
    cq = jnp.einsum("tsd,dw->tsw", scaled, w_q_cross, preferred_element_type=jnp.float32)
    own = rows_reduce_scatter(with_sumsq(cq, residual), seq_dev)
    cross_query = split_norm(own, width).reshape(steps, seq_dev, head_count, DK)
    cross_keys = cross_kv[:, :, 0].reshape(seq_dev, source_len, head_count, DK)
    cross_values = cross_kv[:, :, 1].reshape(seq_dev, source_len, head_count, DK)
    s_cross = jnp.einsum(
        "tnhd,nlhd->tnhl", cross_query, cross_keys, preferred_element_type=jnp.float32
    ) * inv
    w_cross = jnp.where(
        cross_usable[None, :, None, :], score_weight(s_cross), jnp.zeros((), jnp.bfloat16)
    )
    weighted = jnp.einsum(
        "tnhl,nlhd->tnhd", w_cross, cross_values, preferred_element_type=jnp.float32
    )
    totals = jnp.sum(w_cross.astype(jnp.float32), axis=-1)
    context = (weighted / totals[..., None]).reshape(steps, seq_dev, width).astype(jnp.bfloat16)
    context_all = rows_gather(context)
    output_rows = residual + tensor_sum(
        jnp.einsum("tsw,wf->tsf", context_all, w_out_cross, preferred_element_type=jnp.float32)
    )
    return output_rows.astype(jnp.bfloat16)


def solution(mesh):
    in_specs = (
        P(None, "dp", "enc"),
        P(("dp", "enc"), None, None, "tensor"),
        P(("dp", "enc"), None, None, "tensor"),
        P(),
        P(),
        P(),
        P("enc"),
        P("enc", None, "tensor"),
        P("tensor", "enc"),
        P("enc"),
        P("enc", "tensor"),
        P("tensor", "enc"),
    )
    out_specs = P(None, "dp", "enc")
    return jax.shard_map(
        on_device, mesh=mesh, in_specs=in_specs, out_specs=out_specs, check_vma=False
    )
```

```python
import math

import jax
import jax.numpy as jnp
from jax import lax
from jax.sharding import PartitionSpec as P

D = 4096
DK = 256


EPSILON = 1e-06
LANE = 128


def score_weight(scores):
    return jnp.exp(scores).astype(jnp.bfloat16)


def rows_gather(chunk):
    n_enc = lax.axis_size("enc")
    steps, owned, width = chunk.shape
    send = jnp.broadcast_to(chunk[None], (n_enc, steps, owned, width))
    got = lax.all_to_all(send, "enc", 0, 0, tiled=True)
    return got.transpose(1, 0, 2, 3).reshape(steps, n_enc * owned, width)


def tensor_sum(value):
    n_t = lax.axis_size("tensor")
    terms = [value] + [
        lax.ppermute(value, "tensor", [(i, i ^ k) for i in range(n_t)]) for k in range(1, n_t)
    ]
    while len(terms) > 1:
        terms = [terms[k] + terms[k + 1] for k in range(0, len(terms), 2)]
    return terms[0]


def with_sumsq(partial, rows_in):
    squares = jnp.sum(rows_in * rows_in, axis=-1, keepdims=True)
    high = squares.astype(jnp.bfloat16)
    low = (squares - high.astype(jnp.float32)).astype(jnp.bfloat16)
    pad = jnp.zeros(rows_in.shape[:-1] + (LANE - 2,), jnp.bfloat16)
    return jnp.concatenate([partial.astype(jnp.bfloat16), high, low, pad], axis=-1)


def rows_reduce_scatter(partial, owned):
    n_enc = lax.axis_size("enc")
    steps, rows, cols = partial.shape
    send = partial.reshape(steps, n_enc, owned, cols).transpose(1, 0, 2, 3)
    got = lax.all_to_all(send, "enc", 0, 0, tiled=True)
    return jnp.sum(got.astype(jnp.float32), axis=0)


def split_norm(packed, width):
    squares = packed[..., width] + packed[..., width + 1]
    scale = lax.rsqrt(squares / D + EPSILON)
    return (packed[..., :width] * scale[..., None]).astype(jnp.bfloat16)


def exchange_sources(src_pool, assign, my_sources, block_at, enc_at, dp_at, dp_count, enc_count, seq_dev):
    assert seq_dev == dp_count
    my_block = block_at
    source_block = my_sources // seq_dev
    source_row = my_sources % seq_dev
    received = []
    for shift in range(dp_count):
        if shift == 0:
            wanted = my_sources
        else:
            target = (dp_at + shift) % dp_count
            wanted = lax.dynamic_slice_in_dim(
                assign, (target * enc_count + enc_at) * seq_dev, seq_dev
            )
        hit = (wanted // seq_dev) == my_block
        row = jnp.sum(jnp.where(hit, wanted % seq_dev, 0))
        piece = lax.dynamic_index_in_dim(src_pool, row, axis=0, keepdims=False)
        if shift:
            piece = lax.ppermute(
                piece, "dp", [(i, (i + shift) % dp_count) for i in range(dp_count)]
            )
        received.append(piece)
    sender_block = [
        ((dp_at - shift) % dp_count) * enc_count + enc_at for shift in range(dp_count)
    ]
    cross_kv = received[0][None]
    cross_kv = jnp.broadcast_to(cross_kv, (seq_dev,) + cross_kv.shape[1:])
    for shift in range(1, dp_count):
        cross_kv = jnp.where(
            (source_block == sender_block[shift])[:, None, None, None],
            received[shift][None],
            cross_kv,
        )
    return cross_kv


def on_device(
    hidden_in,
    self_cache,
    src_pool,
    assign,
    src_len,
    positions,
    gain_self,
    w_qkv,
    w_out_self,
    gain_cross,
    w_q_cross,
    w_out_cross,
):
    dp_count = lax.axis_size("dp")
    enc_count = lax.axis_size("enc")
    seq_dev = self_cache.shape[0]
    per_pair = seq_dev // dp_count
    cache_len = self_cache.shape[1]
    source_len = src_pool.shape[1]
    width = self_cache.shape[3]
    head_count = width // DK
    steps = hidden_in.shape[0]
    enc_at = lax.axis_index("enc")
    dp_at = lax.axis_index("dp")
    block_at = dp_at * enc_count + enc_at
    slot_index = jnp.arange(seq_dev, dtype=jnp.int32)
    my_slots = block_at * seq_dev + slot_index
    my_positions = lax.dynamic_slice_in_dim(positions, block_at * seq_dev, seq_dev)
    my_sources = lax.dynamic_slice_in_dim(assign, block_at * seq_dev, seq_dev)
    place_at = jnp.arange(cache_len, dtype=jnp.int32)
    cache_usable = place_at[None, :] < my_positions[:, None]
    token_at = jnp.arange(source_len, dtype=jnp.int32)
    source_at = jnp.arange(src_len.shape[0], dtype=jnp.int32)
    my_len = jnp.sum(
        jnp.where(source_at[None, :] == my_sources[:, None], src_len[None, :], 0), axis=1
    )
    cross_usable = token_at[None, :] < my_len[:, None]

    current = hidden_in.astype(jnp.float32)
    scaled = (current * gain_self[None, None, :]).astype(jnp.bfloat16)
    proj = jnp.einsum("tsd,dcw->tscw", scaled, w_qkv, preferred_element_type=jnp.float32)
    proj = proj.reshape(steps, current.shape[1], 3 * width)
    own = rows_reduce_scatter(with_sumsq(proj, current), seq_dev)
    qkv = split_norm(own, 3 * width).reshape(steps, seq_dev, 3, head_count, DK)
    query = qkv[:, :, 0]
    key_new = qkv[:, :, 1]
    value_new = qkv[:, :, 2]

    inv = 1.0 / math.sqrt(DK)
    cache_keys = self_cache[:, :, 0].reshape(seq_dev, cache_len, head_count, DK)
    cache_values = self_cache[:, :, 1].reshape(seq_dev, cache_len, head_count, DK)
    s_cache = jnp.einsum(
        "tnhd,nlhd->tnhl", query, cache_keys, preferred_element_type=jnp.float32
    ) * inv
    w_cache = jnp.where(
        cache_usable[None, :, None, :], score_weight(s_cache), jnp.zeros((), jnp.bfloat16)
    )
    s_new = jnp.einsum(
        "tnhd,unhd->tnhu", query, key_new, preferred_element_type=jnp.float32
    ) * inv
    step_at = jnp.arange(steps, dtype=jnp.int32)
    new_usable = step_at[None, :] <= step_at[:, None]
    w_new = jnp.where(
        new_usable[:, None, None, :], score_weight(s_new), jnp.zeros((), jnp.bfloat16)
    )
    weighted = jnp.einsum(
        "tnhl,nlhd->tnhd", w_cache, cache_values, preferred_element_type=jnp.float32
    ) + jnp.einsum("tnhu,unhd->tnhd", w_new, value_new, preferred_element_type=jnp.float32)
    totals = jnp.sum(w_cache.astype(jnp.float32), axis=-1) + jnp.sum(
        w_new.astype(jnp.float32), axis=-1
    )
    context = (weighted / totals[..., None]).reshape(steps, seq_dev, width).astype(jnp.bfloat16)
    context, src_late = lax.optimization_barrier((context, src_pool))
    cross_kv = exchange_sources(
        src_late, assign, my_sources, block_at, enc_at, dp_at, dp_count, enc_count, seq_dev
    )
    context_all = rows_gather(context)
    residual = current + tensor_sum(
        jnp.einsum("tsw,wf->tsf", context_all, w_out_self, preferred_element_type=jnp.float32)
    )

    scaled = (residual * gain_cross[None, None, :]).astype(jnp.bfloat16)
    cq = jnp.einsum("tsd,dw->tsw", scaled, w_q_cross, preferred_element_type=jnp.float32)
    own = rows_reduce_scatter(with_sumsq(cq, residual), seq_dev)
    cross_query = split_norm(own, width).reshape(steps, seq_dev, head_count, DK)
    cross_keys = cross_kv[:, :, 0].reshape(seq_dev, source_len, head_count, DK)
    cross_values = cross_kv[:, :, 1].reshape(seq_dev, source_len, head_count, DK)
    s_cross = jnp.einsum(
        "tnhd,nlhd->tnhl", cross_query, cross_keys, preferred_element_type=jnp.float32
    ) * inv
    w_cross = jnp.where(
        cross_usable[None, :, None, :], score_weight(s_cross), jnp.zeros((), jnp.bfloat16)
    )
    weighted = jnp.einsum(
        "tnhl,nlhd->tnhd", w_cross, cross_values, preferred_element_type=jnp.float32
    )
    totals = jnp.sum(w_cross.astype(jnp.float32), axis=-1)
    context = (weighted / totals[..., None]).reshape(steps, seq_dev, width).astype(jnp.bfloat16)
    context_all = rows_gather(context)
    output_rows = residual + tensor_sum(
        jnp.einsum("tsw,wf->tsf", context_all, w_out_cross, preferred_element_type=jnp.float32)
    )
    return output_rows.astype(jnp.bfloat16)


def solution(mesh):
    in_specs = (
        P(None, "dp", "enc"),
        P(("dp", "enc"), None, None, "tensor"),
        P(("dp", "enc"), None, None, "tensor"),
        P(),
        P(),
        P(),
        P("enc"),
        P("enc", None, "tensor"),
        P("tensor", "enc"),
        P("enc"),
        P("enc", "tensor"),
        P("tensor", "enc"),
    )
    out_specs = P(None, "dp", "enc")
    return jax.shard_map(
        on_device, mesh=mesh, in_specs=in_specs, out_specs=out_specs, check_vma=False
    )
```

```python
import math

import jax
import jax.numpy as jnp
from jax import lax
from jax.sharding import PartitionSpec as P

D = 4096
DK = 256


EPSILON = 1e-06
LANE = 128


def score_weight(scores):
    return jnp.exp(scores).astype(jnp.bfloat16)


def rows_gather(chunk):
    n_enc = lax.axis_size("enc")
    steps, owned, width = chunk.shape
    send = jnp.broadcast_to(chunk[None], (n_enc, steps, owned, width))
    got = lax.all_to_all(send, "enc", 0, 0, tiled=True)
    return got.transpose(1, 0, 2, 3).reshape(steps, n_enc * owned, width)


def tensor_sum(value):
    n_t = lax.axis_size("tensor")
    value = value.astype(jnp.bfloat16)
    terms = [value] + [
        lax.ppermute(value, "tensor", [(i, i ^ k) for i in range(n_t)]) for k in range(1, n_t)
    ]
    terms = [term.astype(jnp.float32) for term in terms]
    while len(terms) > 1:
        terms = [terms[k] + terms[k + 1] for k in range(0, len(terms), 2)]
    return terms[0]


def with_sumsq(partial, rows_in):
    squares = jnp.sum(rows_in * rows_in, axis=-1, keepdims=True)
    high = squares.astype(jnp.bfloat16)
    low = (squares - high.astype(jnp.float32)).astype(jnp.bfloat16)
    pad = jnp.zeros(rows_in.shape[:-1] + (LANE - 2,), jnp.bfloat16)
    return jnp.concatenate([partial.astype(jnp.bfloat16), high, low, pad], axis=-1)


def rows_reduce_scatter(partial, owned):
    n_enc = lax.axis_size("enc")
    steps, rows, cols = partial.shape
    send = partial.reshape(steps, n_enc, owned, cols).transpose(1, 0, 2, 3)
    got = lax.all_to_all(send, "enc", 0, 0, tiled=True)
    return jnp.sum(got.astype(jnp.float32), axis=0)


def split_norm(packed, width):
    squares = packed[..., width] + packed[..., width + 1]
    scale = lax.rsqrt(squares / D + EPSILON)
    return (packed[..., :width] * scale[..., None]).astype(jnp.bfloat16)


def exchange_sources(src_pool, assign, my_sources, block_at, enc_at, dp_at, dp_count, enc_count, seq_dev):
    assert seq_dev == dp_count
    my_block = block_at
    source_block = my_sources // seq_dev
    source_row = my_sources % seq_dev
    received = []
    for shift in range(dp_count):
        if shift == 0:
            wanted = my_sources
        else:
            target = (dp_at + shift) % dp_count
            wanted = lax.dynamic_slice_in_dim(
                assign, (target * enc_count + enc_at) * seq_dev, seq_dev
            )
        hit = (wanted // seq_dev) == my_block
        row = jnp.sum(jnp.where(hit, wanted % seq_dev, 0))
        piece = lax.dynamic_index_in_dim(src_pool, row, axis=0, keepdims=False)
        if shift:
            piece = lax.ppermute(
                piece, "dp", [(i, (i + shift) % dp_count) for i in range(dp_count)]
            )
        received.append(piece)
    sender_block = [
        ((dp_at - shift) % dp_count) * enc_count + enc_at for shift in range(dp_count)
    ]
    cross_kv = received[0][None]
    cross_kv = jnp.broadcast_to(cross_kv, (seq_dev,) + cross_kv.shape[1:])
    for shift in range(1, dp_count):
        cross_kv = jnp.where(
            (source_block == sender_block[shift])[:, None, None, None],
            received[shift][None],
            cross_kv,
        )
    return cross_kv


def on_device(
    hidden_in,
    self_cache,
    src_pool,
    assign,
    src_len,
    positions,
    gain_self,
    w_qkv,
    w_out_self,
    gain_cross,
    w_q_cross,
    w_out_cross,
):
    dp_count = lax.axis_size("dp")
    enc_count = lax.axis_size("enc")
    seq_dev = self_cache.shape[0]
    per_pair = seq_dev // dp_count
    cache_len = self_cache.shape[1]
    source_len = src_pool.shape[1]
    width = self_cache.shape[3]
    head_count = width // DK
    steps = hidden_in.shape[0]
    enc_at = lax.axis_index("enc")
    dp_at = lax.axis_index("dp")
    block_at = dp_at * enc_count + enc_at
    slot_index = jnp.arange(seq_dev, dtype=jnp.int32)
    my_slots = block_at * seq_dev + slot_index
    my_positions = lax.dynamic_slice_in_dim(positions, block_at * seq_dev, seq_dev)
    my_sources = lax.dynamic_slice_in_dim(assign, block_at * seq_dev, seq_dev)
    place_at = jnp.arange(cache_len, dtype=jnp.int32)
    cache_usable = place_at[None, :] < my_positions[:, None]
    token_at = jnp.arange(source_len, dtype=jnp.int32)
    source_at = jnp.arange(src_len.shape[0], dtype=jnp.int32)
    my_len = jnp.sum(
        jnp.where(source_at[None, :] == my_sources[:, None], src_len[None, :], 0), axis=1
    )
    cross_usable = token_at[None, :] < my_len[:, None]

    current = hidden_in.astype(jnp.float32)
    scaled = (current * gain_self[None, None, :]).astype(jnp.bfloat16)
    proj = jnp.einsum("tsd,dcw->tscw", scaled, w_qkv, preferred_element_type=jnp.float32)
    proj = proj.reshape(steps, current.shape[1], 3 * width)
    own = rows_reduce_scatter(with_sumsq(proj, current), seq_dev)
    qkv = split_norm(own, 3 * width).reshape(steps, seq_dev, 3, head_count, DK)
    query = qkv[:, :, 0]
    key_new = qkv[:, :, 1]
    value_new = qkv[:, :, 2]

    inv = 1.0 / math.sqrt(DK)
    cache_keys = self_cache[:, :, 0].reshape(seq_dev, cache_len, head_count, DK)
    cache_values = self_cache[:, :, 1].reshape(seq_dev, cache_len, head_count, DK)
    s_cache = jnp.einsum(
        "tnhd,nlhd->tnhl", query, cache_keys, preferred_element_type=jnp.float32
    ) * inv
    w_cache = jnp.where(
        cache_usable[None, :, None, :], score_weight(s_cache), jnp.zeros((), jnp.bfloat16)
    )
    s_new = jnp.einsum(
        "tnhd,unhd->tnhu", query, key_new, preferred_element_type=jnp.float32
    ) * inv
    step_at = jnp.arange(steps, dtype=jnp.int32)
    new_usable = step_at[None, :] <= step_at[:, None]
    w_new = jnp.where(
        new_usable[:, None, None, :], score_weight(s_new), jnp.zeros((), jnp.bfloat16)
    )
    weighted = jnp.einsum(
        "tnhl,nlhd->tnhd", w_cache, cache_values, preferred_element_type=jnp.float32
    ) + jnp.einsum("tnhu,unhd->tnhd", w_new, value_new, preferred_element_type=jnp.float32)
    totals = jnp.sum(w_cache.astype(jnp.float32), axis=-1) + jnp.sum(
        w_new.astype(jnp.float32), axis=-1
    )
    context = (weighted / totals[..., None]).reshape(steps, seq_dev, width).astype(jnp.bfloat16)
    context, src_late = lax.optimization_barrier((context, src_pool))
    cross_kv = exchange_sources(
        src_late, assign, my_sources, block_at, enc_at, dp_at, dp_count, enc_count, seq_dev
    )
    context_all = rows_gather(context)
    residual = current + tensor_sum(
        jnp.einsum("tsw,wf->tsf", context_all, w_out_self, preferred_element_type=jnp.float32)
    )

    scaled = (residual * gain_cross[None, None, :]).astype(jnp.bfloat16)
    cq = jnp.einsum("tsd,dw->tsw", scaled, w_q_cross, preferred_element_type=jnp.float32)
    own = rows_reduce_scatter(with_sumsq(cq, residual), seq_dev)
    cross_query = split_norm(own, width).reshape(steps, seq_dev, head_count, DK)
    cross_keys = cross_kv[:, :, 0].reshape(seq_dev, source_len, head_count, DK)
    cross_values = cross_kv[:, :, 1].reshape(seq_dev, source_len, head_count, DK)
    s_cross = jnp.einsum(
        "tnhd,nlhd->tnhl", cross_query, cross_keys, preferred_element_type=jnp.float32
    ) * inv
    w_cross = jnp.where(
        cross_usable[None, :, None, :], score_weight(s_cross), jnp.zeros((), jnp.bfloat16)
    )
    weighted = jnp.einsum(
        "tnhl,nlhd->tnhd", w_cross, cross_values, preferred_element_type=jnp.float32
    )
    totals = jnp.sum(w_cross.astype(jnp.float32), axis=-1)
    context = (weighted / totals[..., None]).reshape(steps, seq_dev, width).astype(jnp.bfloat16)
    context_all = rows_gather(context)
    output_rows = residual + tensor_sum(
        jnp.einsum("tsw,wf->tsf", context_all, w_out_cross, preferred_element_type=jnp.float32)
    )
    return output_rows.astype(jnp.bfloat16)


def solution(mesh):
    in_specs = (
        P(None, "dp", "enc"),
        P(("dp", "enc"), None, None, "tensor"),
        P(("dp", "enc"), None, None, "tensor"),
        P(),
        P(),
        P(),
        P("enc"),
        P("enc", None, "tensor"),
        P("tensor", "enc"),
        P("enc"),
        P("enc", "tensor"),
        P("tensor", "enc"),
    )
    out_specs = P(None, "dp", "enc")
    return jax.shard_map(
        on_device, mesh=mesh, in_specs=in_specs, out_specs=out_specs, check_vma=False
    )
```

```python
import math

import jax
import jax.numpy as jnp
from jax import lax
from jax.sharding import PartitionSpec as P

D = 4096
DK = 256


EPSILON = 1e-06
LANE = 128


def score_weight(scores):
    return jnp.exp(scores).astype(jnp.bfloat16)


def rows_gather(chunk):
    n_enc = lax.axis_size("enc")
    steps, owned, width = chunk.shape
    send = jnp.broadcast_to(chunk[None], (n_enc, steps, owned, width))
    got = lax.all_to_all(send, "enc", 0, 0, tiled=True)
    return got.transpose(1, 0, 2, 3).reshape(steps, n_enc * owned, width)


def tensor_sum(value):
    n_t = lax.axis_size("tensor")
    value = value.astype(jnp.bfloat16)
    terms = [value] + [
        lax.ppermute(value, "tensor", [(i, i ^ k) for i in range(n_t)]) for k in range(1, n_t)
    ]
    terms = [term.astype(jnp.float32) for term in terms]
    while len(terms) > 1:
        terms = [terms[k] + terms[k + 1] for k in range(0, len(terms), 2)]
    return terms[0]


def with_sumsq(partial, rows_in):
    squares = jnp.sum(rows_in * rows_in, axis=-1, keepdims=True)
    high = squares.astype(jnp.bfloat16)
    low = (squares - high.astype(jnp.float32)).astype(jnp.bfloat16)
    pad = jnp.zeros(rows_in.shape[:-1] + (LANE - 2,), jnp.bfloat16)
    return jnp.concatenate([partial.astype(jnp.bfloat16), high, low, pad], axis=-1)


def rows_reduce_scatter(partial, owned):
    n_enc = lax.axis_size("enc")
    steps, rows, cols = partial.shape
    send = partial.reshape(steps, n_enc, owned, cols).transpose(1, 0, 2, 3)
    got = lax.all_to_all(send, "enc", 0, 0, tiled=True)
    return jnp.sum(got.astype(jnp.float32), axis=0)


def split_norm(packed, width):
    squares = packed[..., width] + packed[..., width + 1]
    scale = lax.rsqrt(squares / D + EPSILON)
    return (packed[..., :width] * scale[..., None]).astype(jnp.bfloat16)


def exchange_sources(src_pool, assign, my_sources, block_at, enc_at, dp_at, dp_count, enc_count, seq_dev):
    assert seq_dev == dp_count
    my_block = block_at
    source_block = my_sources // seq_dev
    source_row = my_sources % seq_dev
    received = []
    for shift in range(dp_count):
        if shift == 0:
            wanted = my_sources
        else:
            target = (dp_at + shift) % dp_count
            wanted = lax.dynamic_slice_in_dim(
                assign, (target * enc_count + enc_at) * seq_dev, seq_dev
            )
        hit = (wanted // seq_dev) == my_block
        row = jnp.sum(jnp.where(hit, wanted % seq_dev, 0))
        piece = lax.dynamic_index_in_dim(src_pool, row, axis=0, keepdims=False)
        if shift:
            piece = lax.ppermute(
                piece, "dp", [(i, (i + shift) % dp_count) for i in range(dp_count)]
            )
        received.append(piece)
    sender_block = [
        ((dp_at - shift) % dp_count) * enc_count + enc_at for shift in range(dp_count)
    ]
    cross_kv = received[0][None]
    cross_kv = jnp.broadcast_to(cross_kv, (seq_dev,) + cross_kv.shape[1:])
    for shift in range(1, dp_count):
        cross_kv = jnp.where(
            (source_block == sender_block[shift])[:, None, None, None],
            received[shift][None],
            cross_kv,
        )
    return cross_kv


def on_device(
    hidden_in,
    self_cache,
    src_pool,
    assign,
    src_len,
    positions,
    gain_self,
    w_qkv,
    w_out_self,
    gain_cross,
    w_q_cross,
    w_out_cross,
):
    dp_count = lax.axis_size("dp")
    enc_count = lax.axis_size("enc")
    seq_dev = self_cache.shape[0]
    per_pair = seq_dev // dp_count
    cache_len = self_cache.shape[1]
    source_len = src_pool.shape[1]
    width = self_cache.shape[3]
    head_count = width // DK
    steps = hidden_in.shape[0]
    enc_at = lax.axis_index("enc")
    dp_at = lax.axis_index("dp")
    block_at = dp_at * enc_count + enc_at
    slot_index = jnp.arange(seq_dev, dtype=jnp.int32)
    my_slots = block_at * seq_dev + slot_index
    my_positions = lax.dynamic_slice_in_dim(positions, block_at * seq_dev, seq_dev)
    my_sources = lax.dynamic_slice_in_dim(assign, block_at * seq_dev, seq_dev)
    place_at = jnp.arange(cache_len, dtype=jnp.int32)
    cache_usable = place_at[None, :] < my_positions[:, None]
    token_at = jnp.arange(source_len, dtype=jnp.int32)
    source_at = jnp.arange(src_len.shape[0], dtype=jnp.int32)
    my_len = jnp.sum(
        jnp.where(source_at[None, :] == my_sources[:, None], src_len[None, :], 0), axis=1
    )
    cross_usable = token_at[None, :] < my_len[:, None]

    w_q_gained = (gain_cross[:, None] * w_q_cross.astype(jnp.float32)).astype(jnp.bfloat16)

    current = hidden_in.astype(jnp.float32)
    scaled = (current * gain_self[None, None, :]).astype(jnp.bfloat16)
    proj = jnp.einsum("tsd,dcw->tscw", scaled, w_qkv, preferred_element_type=jnp.float32)
    proj = proj.reshape(steps, current.shape[1], 3 * width)
    own = rows_reduce_scatter(with_sumsq(proj, current), seq_dev)
    qkv = split_norm(own, 3 * width).reshape(steps, seq_dev, 3, head_count, DK)
    query = qkv[:, :, 0]
    key_new = qkv[:, :, 1]
    value_new = qkv[:, :, 2]

    inv = 1.0 / math.sqrt(DK)
    cache_keys = self_cache[:, :, 0].reshape(seq_dev, cache_len, head_count, DK)
    cache_values = self_cache[:, :, 1].reshape(seq_dev, cache_len, head_count, DK)
    s_cache = jnp.einsum(
        "tnhd,nlhd->tnhl", query, cache_keys, preferred_element_type=jnp.float32
    ) * inv
    w_cache = jnp.where(
        cache_usable[None, :, None, :], score_weight(s_cache), jnp.zeros((), jnp.bfloat16)
    )
    s_new = jnp.einsum(
        "tnhd,unhd->tnhu", query, key_new, preferred_element_type=jnp.float32
    ) * inv
    step_at = jnp.arange(steps, dtype=jnp.int32)
    new_usable = step_at[None, :] <= step_at[:, None]
    w_new = jnp.where(
        new_usable[:, None, None, :], score_weight(s_new), jnp.zeros((), jnp.bfloat16)
    )
    weighted = jnp.einsum(
        "tnhl,nlhd->tnhd", w_cache, cache_values, preferred_element_type=jnp.float32
    ) + jnp.einsum("tnhu,unhd->tnhd", w_new, value_new, preferred_element_type=jnp.float32)
    totals = jnp.sum(w_cache.astype(jnp.float32), axis=-1) + jnp.sum(
        w_new.astype(jnp.float32), axis=-1
    )
    context = (weighted / totals[..., None]).reshape(steps, seq_dev, width).astype(jnp.bfloat16)
    context, src_late, w_q_gained = lax.optimization_barrier((context, src_pool, w_q_gained))
    cross_kv = exchange_sources(
        src_late, assign, my_sources, block_at, enc_at, dp_at, dp_count, enc_count, seq_dev
    )
    context_all = rows_gather(context)
    residual = current + tensor_sum(
        jnp.einsum("tsw,wf->tsf", context_all, w_out_self, preferred_element_type=jnp.float32)
    )

    cq = jnp.einsum(
        "tsd,dw->tsw", residual.astype(jnp.bfloat16), w_q_gained, preferred_element_type=jnp.float32
    )
    own = rows_reduce_scatter(with_sumsq(cq, residual), seq_dev)
    cross_query = split_norm(own, width).reshape(steps, seq_dev, head_count, DK)
    cross_keys = cross_kv[:, :, 0].reshape(seq_dev, source_len, head_count, DK)
    cross_values = cross_kv[:, :, 1].reshape(seq_dev, source_len, head_count, DK)
    s_cross = jnp.einsum(
        "tnhd,nlhd->tnhl", cross_query, cross_keys, preferred_element_type=jnp.float32
    ) * inv
    w_cross = jnp.where(
        cross_usable[None, :, None, :], score_weight(s_cross), jnp.zeros((), jnp.bfloat16)
    )
    weighted = jnp.einsum(
        "tnhl,nlhd->tnhd", w_cross, cross_values, preferred_element_type=jnp.float32
    )
    totals = jnp.sum(w_cross.astype(jnp.float32), axis=-1)
    context = (weighted / totals[..., None]).reshape(steps, seq_dev, width).astype(jnp.bfloat16)
    context_all = rows_gather(context)
    output_rows = residual + tensor_sum(
        jnp.einsum("tsw,wf->tsf", context_all, w_out_cross, preferred_element_type=jnp.float32)
    )
    return output_rows.astype(jnp.bfloat16)


def solution(mesh):
    in_specs = (
        P(None, "dp", "enc"),
        P(("dp", "enc"), None, None, "tensor"),
        P(("dp", "enc"), None, None, "tensor"),
        P(),
        P(),
        P(),
        P("enc"),
        P("enc", None, "tensor"),
        P("tensor", "enc"),
        P("enc"),
        P("enc", "tensor"),
        P("tensor", "enc"),
    )
    out_specs = P(None, "dp", "enc")
    return jax.shard_map(
        on_device, mesh=mesh, in_specs=in_specs, out_specs=out_specs, check_vma=False
    )
```

```python
import math

import jax
import jax.numpy as jnp
from jax import lax
from jax.sharding import PartitionSpec as P

D = 4096
DK = 256


EPSILON = 1e-06
LANE = 128


def score_weight(scores):
    return jnp.exp(scores).astype(jnp.bfloat16)


def rows_gather(chunk):
    n_enc = lax.axis_size("enc")
    steps, owned, width = chunk.shape
    send = jnp.broadcast_to(chunk[None], (n_enc, steps, owned, width))
    got = lax.all_to_all(send, "enc", 0, 0, tiled=True)
    return got.transpose(1, 0, 2, 3).reshape(steps, n_enc * owned, width)


def tensor_sum(value):
    n_t = lax.axis_size("tensor")
    value = value.astype(jnp.bfloat16)
    terms = [value] + [
        lax.ppermute(value, "tensor", [(i, i ^ k) for i in range(n_t)]) for k in range(1, n_t)
    ]
    terms = [term.astype(jnp.float32) for term in terms]
    while len(terms) > 1:
        terms = [terms[k] + terms[k + 1] for k in range(0, len(terms), 2)]
    return terms[0]


def with_sumsq(partial, rows_in):
    squares = jnp.sum(rows_in * rows_in, axis=-1, keepdims=True)
    high = squares.astype(jnp.bfloat16)
    low = jnp.where(
        jnp.isfinite(squares), squares - high.astype(jnp.float32), 0.0
    ).astype(jnp.bfloat16)
    pad = jnp.zeros(rows_in.shape[:-1] + (LANE - 2,), jnp.bfloat16)
    return jnp.concatenate([partial.astype(jnp.bfloat16), high, low, pad], axis=-1)


def rows_reduce_scatter(partial, owned):
    n_enc = lax.axis_size("enc")
    steps, rows, cols = partial.shape
    send = partial.reshape(steps, n_enc, owned, cols).transpose(1, 0, 2, 3)
    got = lax.all_to_all(send, "enc", 0, 0, tiled=True)
    return jnp.sum(got.astype(jnp.float32), axis=0)


def split_norm(packed, width):
    squares = packed[..., width] + packed[..., width + 1]
    scale = lax.rsqrt(squares / D + EPSILON)
    return (packed[..., :width] * scale[..., None]).astype(jnp.bfloat16)


def exchange_sources(src_pool, assign, my_sources, block_at, enc_at, dp_at, dp_count, enc_count, seq_dev):
    assert seq_dev == dp_count
    my_block = block_at
    source_block = my_sources // seq_dev
    source_row = my_sources % seq_dev
    received = []
    for shift in range(dp_count):
        if shift == 0:
            wanted = my_sources
        else:
            target = (dp_at + shift) % dp_count
            wanted = lax.dynamic_slice_in_dim(
                assign, (target * enc_count + enc_at) * seq_dev, seq_dev
            )
        hit = (wanted // seq_dev) == my_block
        row = jnp.sum(jnp.where(hit, wanted % seq_dev, 0))
        piece = lax.dynamic_index_in_dim(src_pool, row, axis=0, keepdims=False)
        if shift:
            piece = lax.ppermute(
                piece, "dp", [(i, (i + shift) % dp_count) for i in range(dp_count)]
            )
        received.append(piece)
    sender_block = [
        ((dp_at - shift) % dp_count) * enc_count + enc_at for shift in range(dp_count)
    ]
    cross_kv = received[0][None]
    cross_kv = jnp.broadcast_to(cross_kv, (seq_dev,) + cross_kv.shape[1:])
    for shift in range(1, dp_count):
        cross_kv = jnp.where(
            (source_block == sender_block[shift])[:, None, None, None],
            received[shift][None],
            cross_kv,
        )
    return cross_kv


def on_device(
    hidden_in,
    self_cache,
    src_pool,
    assign,
    src_len,
    positions,
    gain_self,
    w_qkv,
    w_out_self,
    gain_cross,
    w_q_cross,
    w_out_cross,
):
    dp_count = lax.axis_size("dp")
    enc_count = lax.axis_size("enc")
    seq_dev = self_cache.shape[0]
    per_pair = seq_dev // dp_count
    cache_len = self_cache.shape[1]
    source_len = src_pool.shape[1]
    width = self_cache.shape[3]
    head_count = width // DK
    steps = hidden_in.shape[0]
    enc_at = lax.axis_index("enc")
    dp_at = lax.axis_index("dp")
    block_at = dp_at * enc_count + enc_at
    slot_index = jnp.arange(seq_dev, dtype=jnp.int32)
    my_slots = block_at * seq_dev + slot_index
    my_positions = lax.dynamic_slice_in_dim(positions, block_at * seq_dev, seq_dev)
    my_sources = lax.dynamic_slice_in_dim(assign, block_at * seq_dev, seq_dev)
    place_at = jnp.arange(cache_len, dtype=jnp.int32)
    cache_usable = place_at[None, :] < my_positions[:, None]
    token_at = jnp.arange(source_len, dtype=jnp.int32)
    source_at = jnp.arange(src_len.shape[0], dtype=jnp.int32)
    my_len = jnp.sum(
        jnp.where(source_at[None, :] == my_sources[:, None], src_len[None, :], 0), axis=1
    )
    cross_usable = token_at[None, :] < my_len[:, None]

    current = hidden_in.astype(jnp.float32)
    scaled = (current * gain_self[None, None, :]).astype(jnp.bfloat16)
    proj = jnp.einsum("tsd,dcw->tscw", scaled, w_qkv, preferred_element_type=jnp.float32)
    proj = proj.reshape(steps, current.shape[1], 3 * width)
    own = rows_reduce_scatter(with_sumsq(proj, current), seq_dev)
    qkv = split_norm(own, 3 * width).reshape(steps, seq_dev, 3, head_count, DK)
    query = qkv[:, :, 0]
    key_new = qkv[:, :, 1]
    value_new = qkv[:, :, 2]

    inv = 1.0 / math.sqrt(DK)
    cache_keys = self_cache[:, :, 0].reshape(seq_dev, cache_len, head_count, DK)
    cache_values = self_cache[:, :, 1].reshape(seq_dev, cache_len, head_count, DK)
    s_cache = jnp.einsum(
        "tnhd,nlhd->tnhl", query, cache_keys, preferred_element_type=jnp.float32
    ) * inv
    w_cache = jnp.where(
        cache_usable[None, :, None, :], score_weight(s_cache), jnp.zeros((), jnp.bfloat16)
    )
    s_new = jnp.einsum(
        "tnhd,unhd->tnhu", query, key_new, preferred_element_type=jnp.float32
    ) * inv
    step_at = jnp.arange(steps, dtype=jnp.int32)
    new_usable = step_at[None, :] <= step_at[:, None]
    w_new = jnp.where(
        new_usable[:, None, None, :], score_weight(s_new), jnp.zeros((), jnp.bfloat16)
    )
    weighted = jnp.einsum(
        "tnhl,nlhd->tnhd", w_cache, cache_values, preferred_element_type=jnp.float32
    ) + jnp.einsum("tnhu,unhd->tnhd", w_new, value_new, preferred_element_type=jnp.float32)
    totals = jnp.sum(w_cache.astype(jnp.float32), axis=-1) + jnp.sum(
        w_new.astype(jnp.float32), axis=-1
    )
    context = (weighted / totals[..., None]).reshape(steps, seq_dev, width).astype(jnp.bfloat16)
    context, src_late = lax.optimization_barrier((context, src_pool))
    cross_kv = exchange_sources(
        src_late, assign, my_sources, block_at, enc_at, dp_at, dp_count, enc_count, seq_dev
    )
    context_all = rows_gather(context)
    residual = current + tensor_sum(
        jnp.einsum("tsw,wf->tsf", context_all, w_out_self, preferred_element_type=jnp.float32)
    )

    scaled = (residual * gain_cross[None, None, :]).astype(jnp.bfloat16)
    cq = jnp.einsum("tsd,dw->tsw", scaled, w_q_cross, preferred_element_type=jnp.float32)
    own = rows_reduce_scatter(with_sumsq(cq, residual), seq_dev)
    cross_query = split_norm(own, width).reshape(steps, seq_dev, head_count, DK)
    cross_keys = cross_kv[:, :, 0].reshape(seq_dev, source_len, head_count, DK)
    cross_values = cross_kv[:, :, 1].reshape(seq_dev, source_len, head_count, DK)
    s_cross = jnp.einsum(
        "tnhd,nlhd->tnhl", cross_query, cross_keys, preferred_element_type=jnp.float32
    ) * inv
    w_cross = jnp.where(
        cross_usable[None, :, None, :], score_weight(s_cross), jnp.zeros((), jnp.bfloat16)
    )
    weighted = jnp.einsum(
        "tnhl,nlhd->tnhd", w_cross, cross_values, preferred_element_type=jnp.float32
    )
    totals = jnp.sum(w_cross.astype(jnp.float32), axis=-1)
    context = (weighted / totals[..., None]).reshape(steps, seq_dev, width).astype(jnp.bfloat16)
    context_all = rows_gather(context)
    output_rows = residual + tensor_sum(
        jnp.einsum("tsw,wf->tsf", context_all, w_out_cross, preferred_element_type=jnp.float32)
    )
    return output_rows.astype(jnp.bfloat16)


def solution(mesh):
    in_specs = (
        P(None, "dp", "enc"),
        P(("dp", "enc"), None, None, "tensor"),
        P(("dp", "enc"), None, None, "tensor"),
        P(),
        P(),
        P(),
        P("enc"),
        P("enc", None, "tensor"),
        P("tensor", "enc"),
        P("enc"),
        P("enc", "tensor"),
        P("tensor", "enc"),
    )
    out_specs = P(None, "dp", "enc")
    return jax.shard_map(
        on_device, mesh=mesh, in_specs=in_specs, out_specs=out_specs, check_vma=False
    )
```

```python
import math

import jax
import jax.numpy as jnp
from jax import lax
from jax.sharding import PartitionSpec as P

D = 4096
DK = 256


EPSILON = 1e-06
LANE = 128


def score_weight(scores):
    return jnp.exp(scores).astype(jnp.bfloat16)


def rows_gather(chunk):
    n_enc = lax.axis_size("enc")
    steps, owned, width = chunk.shape
    send = jnp.broadcast_to(chunk[None], (n_enc, steps, owned, width))
    got = lax.all_to_all(send, "enc", 0, 0, tiled=True)
    return got.transpose(1, 0, 2, 3).reshape(steps, n_enc * owned, width)


def tensor_sum(value):
    n_t = lax.axis_size("tensor")
    value = value.astype(jnp.bfloat16)
    terms = [value] + [
        lax.ppermute(value, "tensor", [(i, i ^ k) for i in range(n_t)]) for k in range(1, n_t)
    ]
    terms = [term.astype(jnp.float32) for term in terms]
    while len(terms) > 1:
        terms = [terms[k] + terms[k + 1] for k in range(0, len(terms), 2)]
    return terms[0]


def with_sumsq(partial, rows_in):
    sq = rows_in * rows_in
    sq_high = sq.astype(jnp.bfloat16)
    sq_low = (sq - sq_high.astype(jnp.float32)).astype(jnp.bfloat16)
    ones = jnp.ones((sq.shape[-1], 1), jnp.bfloat16)
    squares = jnp.dot(sq_high, ones, preferred_element_type=jnp.float32) + jnp.dot(
        sq_low, ones, preferred_element_type=jnp.float32
    )
    high = squares.astype(jnp.bfloat16)
    low = jnp.where(
        jnp.isfinite(squares), squares - high.astype(jnp.float32), 0.0
    ).astype(jnp.bfloat16)
    pad = jnp.zeros(rows_in.shape[:-1] + (LANE - 2,), jnp.bfloat16)
    return jnp.concatenate([partial.astype(jnp.bfloat16), high, low, pad], axis=-1)


def rows_reduce_scatter(partial, owned):
    n_enc = lax.axis_size("enc")
    steps, rows, cols = partial.shape
    send = partial.reshape(steps, n_enc, owned, cols).transpose(1, 0, 2, 3)
    got = lax.all_to_all(send, "enc", 0, 0, tiled=True)
    return jnp.sum(got.astype(jnp.float32), axis=0)


def split_norm(packed, width):
    squares = packed[..., width] + packed[..., width + 1]
    scale = lax.rsqrt(squares / D + EPSILON)
    return (packed[..., :width] * scale[..., None]).astype(jnp.bfloat16)


def exchange_sources(src_pool, assign, my_sources, block_at, enc_at, dp_at, dp_count, enc_count, seq_dev):
    assert seq_dev == dp_count
    my_block = block_at
    source_block = my_sources // seq_dev
    source_row = my_sources % seq_dev
    received = []
    for shift in range(dp_count):
        if shift == 0:
            wanted = my_sources
        else:
            target = (dp_at + shift) % dp_count
            wanted = lax.dynamic_slice_in_dim(
                assign, (target * enc_count + enc_at) * seq_dev, seq_dev
            )
        hit = (wanted // seq_dev) == my_block
        row = jnp.sum(jnp.where(hit, wanted % seq_dev, 0))
        piece = lax.dynamic_index_in_dim(src_pool, row, axis=0, keepdims=False)
        if shift:
            piece = lax.ppermute(
                piece, "dp", [(i, (i + shift) % dp_count) for i in range(dp_count)]
            )
        received.append(piece)
    sender_block = [
        ((dp_at - shift) % dp_count) * enc_count + enc_at for shift in range(dp_count)
    ]
    cross_kv = received[0][None]
    cross_kv = jnp.broadcast_to(cross_kv, (seq_dev,) + cross_kv.shape[1:])
    for shift in range(1, dp_count):
        cross_kv = jnp.where(
            (source_block == sender_block[shift])[:, None, None, None],
            received[shift][None],
            cross_kv,
        )
    return cross_kv


def on_device(
    hidden_in,
    self_cache,
    src_pool,
    assign,
    src_len,
    positions,
    gain_self,
    w_qkv,
    w_out_self,
    gain_cross,
    w_q_cross,
    w_out_cross,
):
    dp_count = lax.axis_size("dp")
    enc_count = lax.axis_size("enc")
    seq_dev = self_cache.shape[0]
    per_pair = seq_dev // dp_count
    cache_len = self_cache.shape[1]
    source_len = src_pool.shape[1]
    width = self_cache.shape[3]
    head_count = width // DK
    steps = hidden_in.shape[0]
    enc_at = lax.axis_index("enc")
    dp_at = lax.axis_index("dp")
    block_at = dp_at * enc_count + enc_at
    slot_index = jnp.arange(seq_dev, dtype=jnp.int32)
    my_slots = block_at * seq_dev + slot_index
    my_positions = lax.dynamic_slice_in_dim(positions, block_at * seq_dev, seq_dev)
    my_sources = lax.dynamic_slice_in_dim(assign, block_at * seq_dev, seq_dev)
    place_at = jnp.arange(cache_len, dtype=jnp.int32)
    cache_usable = place_at[None, :] < my_positions[:, None]
    token_at = jnp.arange(source_len, dtype=jnp.int32)
    source_at = jnp.arange(src_len.shape[0], dtype=jnp.int32)
    my_len = jnp.sum(
        jnp.where(source_at[None, :] == my_sources[:, None], src_len[None, :], 0), axis=1
    )
    cross_usable = token_at[None, :] < my_len[:, None]

    current = hidden_in.astype(jnp.float32)
    scaled = (current * gain_self[None, None, :]).astype(jnp.bfloat16)
    proj = jnp.einsum("tsd,dcw->tscw", scaled, w_qkv, preferred_element_type=jnp.float32)
    proj = proj.reshape(steps, current.shape[1], 3 * width)
    own = rows_reduce_scatter(with_sumsq(proj, current), seq_dev)
    qkv = split_norm(own, 3 * width).reshape(steps, seq_dev, 3, head_count, DK)
    query = qkv[:, :, 0]
    key_new = qkv[:, :, 1]
    value_new = qkv[:, :, 2]

    inv = 1.0 / math.sqrt(DK)
    cache_keys = self_cache[:, :, 0].reshape(seq_dev, cache_len, head_count, DK)
    cache_values = self_cache[:, :, 1].reshape(seq_dev, cache_len, head_count, DK)
    s_cache = jnp.einsum(
        "tnhd,nlhd->tnhl", query, cache_keys, preferred_element_type=jnp.float32
    ) * inv
    w_cache = jnp.where(
        cache_usable[None, :, None, :], score_weight(s_cache), jnp.zeros((), jnp.bfloat16)
    )
    s_new = jnp.einsum(
        "tnhd,unhd->tnhu", query, key_new, preferred_element_type=jnp.float32
    ) * inv
    step_at = jnp.arange(steps, dtype=jnp.int32)
    new_usable = step_at[None, :] <= step_at[:, None]
    w_new = jnp.where(
        new_usable[:, None, None, :], score_weight(s_new), jnp.zeros((), jnp.bfloat16)
    )
    weighted = jnp.einsum(
        "tnhl,nlhd->tnhd", w_cache, cache_values, preferred_element_type=jnp.float32
    ) + jnp.einsum("tnhu,unhd->tnhd", w_new, value_new, preferred_element_type=jnp.float32)
    totals = jnp.sum(w_cache.astype(jnp.float32), axis=-1) + jnp.sum(
        w_new.astype(jnp.float32), axis=-1
    )
    context = (weighted / totals[..., None]).reshape(steps, seq_dev, width).astype(jnp.bfloat16)
    context, src_late = lax.optimization_barrier((context, src_pool))
    cross_kv = exchange_sources(
        src_late, assign, my_sources, block_at, enc_at, dp_at, dp_count, enc_count, seq_dev
    )
    context_all = rows_gather(context)
    residual = current + tensor_sum(
        jnp.einsum("tsw,wf->tsf", context_all, w_out_self, preferred_element_type=jnp.float32)
    )

    scaled = (residual * gain_cross[None, None, :]).astype(jnp.bfloat16)
    cq = jnp.einsum("tsd,dw->tsw", scaled, w_q_cross, preferred_element_type=jnp.float32)
    own = rows_reduce_scatter(with_sumsq(cq, residual), seq_dev)
    cross_query = split_norm(own, width).reshape(steps, seq_dev, head_count, DK)
    cross_keys = cross_kv[:, :, 0].reshape(seq_dev, source_len, head_count, DK)
    cross_values = cross_kv[:, :, 1].reshape(seq_dev, source_len, head_count, DK)
    s_cross = jnp.einsum(
        "tnhd,nlhd->tnhl", cross_query, cross_keys, preferred_element_type=jnp.float32
    ) * inv
    w_cross = jnp.where(
        cross_usable[None, :, None, :], score_weight(s_cross), jnp.zeros((), jnp.bfloat16)
    )
    weighted = jnp.einsum(
        "tnhl,nlhd->tnhd", w_cross, cross_values, preferred_element_type=jnp.float32
    )
    totals = jnp.sum(w_cross.astype(jnp.float32), axis=-1)
    context = (weighted / totals[..., None]).reshape(steps, seq_dev, width).astype(jnp.bfloat16)
    context_all = rows_gather(context)
    output_rows = residual + tensor_sum(
        jnp.einsum("tsw,wf->tsf", context_all, w_out_cross, preferred_element_type=jnp.float32)
    )
    return output_rows.astype(jnp.bfloat16)


def solution(mesh):
    in_specs = (
        P(None, "dp", "enc"),
        P(("dp", "enc"), None, None, "tensor"),
        P(("dp", "enc"), None, None, "tensor"),
        P(),
        P(),
        P(),
        P("enc"),
        P("enc", None, "tensor"),
        P("tensor", "enc"),
        P("enc"),
        P("enc", "tensor"),
        P("tensor", "enc"),
    )
    out_specs = P(None, "dp", "enc")
    return jax.shard_map(
        on_device, mesh=mesh, in_specs=in_specs, out_specs=out_specs, check_vma=False
    )
```

```python
import math

import jax
import jax.numpy as jnp
from jax import lax
from jax.sharding import PartitionSpec as P

D = 4096
DK = 256


EPSILON = 1e-06
LANE = 128


def score_weight(scores):
    return jnp.exp(scores).astype(jnp.bfloat16)


def rows_gather(chunk):
    n_enc = lax.axis_size("enc")
    steps, owned, width = chunk.shape
    send = jnp.broadcast_to(chunk[None], (n_enc, steps, owned, width))
    got = lax.all_to_all(send, "enc", 0, 0, tiled=True)
    return got.transpose(1, 0, 2, 3).reshape(steps, n_enc * owned, width)


def tensor_sum(value):
    n_t = lax.axis_size("tensor")
    value = value.astype(jnp.bfloat16).astype(jnp.float32)
    bit = 1
    while bit < n_t:
        sent = value.astype(jnp.bfloat16) if bit == 1 else value
        other = lax.ppermute(sent, "tensor", [(i, i ^ bit) for i in range(n_t)])
        value = value + other.astype(jnp.float32)
        bit *= 2
    return value


def with_sumsq(partial, rows_in):
    squares = jnp.sum(rows_in * rows_in, axis=-1, keepdims=True)
    high = squares.astype(jnp.bfloat16)
    low = jnp.where(
        jnp.isfinite(squares), squares - high.astype(jnp.float32), 0.0
    ).astype(jnp.bfloat16)
    pad = jnp.zeros(rows_in.shape[:-1] + (LANE - 2,), jnp.bfloat16)
    return jnp.concatenate([partial.astype(jnp.bfloat16), high, low, pad], axis=-1)


def rows_reduce_scatter(partial, owned):
    n_enc = lax.axis_size("enc")
    steps, rows, cols = partial.shape
    send = partial.reshape(steps, n_enc, owned, cols).transpose(1, 0, 2, 3)
    got = lax.all_to_all(send, "enc", 0, 0, tiled=True)
    return jnp.sum(got.astype(jnp.float32), axis=0)


def split_norm(packed, width):
    squares = packed[..., width] + packed[..., width + 1]
    scale = lax.rsqrt(squares / D + EPSILON)
    return (packed[..., :width] * scale[..., None]).astype(jnp.bfloat16)


def exchange_sources(src_pool, assign, my_sources, block_at, enc_at, dp_at, dp_count, enc_count, seq_dev):
    assert seq_dev == dp_count
    my_block = block_at
    source_block = my_sources // seq_dev
    source_row = my_sources % seq_dev
    received = []
    for shift in range(dp_count):
        if shift == 0:
            wanted = my_sources
        else:
            target = (dp_at + shift) % dp_count
            wanted = lax.dynamic_slice_in_dim(
                assign, (target * enc_count + enc_at) * seq_dev, seq_dev
            )
        hit = (wanted // seq_dev) == my_block
        row = jnp.sum(jnp.where(hit, wanted % seq_dev, 0))
        piece = lax.dynamic_index_in_dim(src_pool, row, axis=0, keepdims=False)
        if shift:
            piece = lax.ppermute(
                piece, "dp", [(i, (i + shift) % dp_count) for i in range(dp_count)]
            )
        received.append(piece)
    sender_block = [
        ((dp_at - shift) % dp_count) * enc_count + enc_at for shift in range(dp_count)
    ]
    cross_kv = received[0][None]
    cross_kv = jnp.broadcast_to(cross_kv, (seq_dev,) + cross_kv.shape[1:])
    for shift in range(1, dp_count):
        cross_kv = jnp.where(
            (source_block == sender_block[shift])[:, None, None, None],
            received[shift][None],
            cross_kv,
        )
    return cross_kv


def on_device(
    hidden_in,
    self_cache,
    src_pool,
    assign,
    src_len,
    positions,
    gain_self,
    w_qkv,
    w_out_self,
    gain_cross,
    w_q_cross,
    w_out_cross,
):
    dp_count = lax.axis_size("dp")
    enc_count = lax.axis_size("enc")
    seq_dev = self_cache.shape[0]
    per_pair = seq_dev // dp_count
    cache_len = self_cache.shape[1]
    source_len = src_pool.shape[1]
    width = self_cache.shape[3]
    head_count = width // DK
    steps = hidden_in.shape[0]
    enc_at = lax.axis_index("enc")
    dp_at = lax.axis_index("dp")
    block_at = dp_at * enc_count + enc_at
    slot_index = jnp.arange(seq_dev, dtype=jnp.int32)
    my_slots = block_at * seq_dev + slot_index
    my_positions = lax.dynamic_slice_in_dim(positions, block_at * seq_dev, seq_dev)
    my_sources = lax.dynamic_slice_in_dim(assign, block_at * seq_dev, seq_dev)
    place_at = jnp.arange(cache_len, dtype=jnp.int32)
    cache_usable = place_at[None, :] < my_positions[:, None]
    token_at = jnp.arange(source_len, dtype=jnp.int32)
    source_at = jnp.arange(src_len.shape[0], dtype=jnp.int32)
    my_len = jnp.sum(
        jnp.where(source_at[None, :] == my_sources[:, None], src_len[None, :], 0), axis=1
    )
    cross_usable = token_at[None, :] < my_len[:, None]

    current = hidden_in.astype(jnp.float32)
    scaled = (current * gain_self[None, None, :]).astype(jnp.bfloat16)
    proj = jnp.einsum("tsd,dcw->tscw", scaled, w_qkv, preferred_element_type=jnp.float32)
    proj = proj.reshape(steps, current.shape[1], 3 * width)
    own = rows_reduce_scatter(with_sumsq(proj, current), seq_dev)
    qkv = split_norm(own, 3 * width).reshape(steps, seq_dev, 3, head_count, DK)
    query = qkv[:, :, 0]
    key_new = qkv[:, :, 1]
    value_new = qkv[:, :, 2]

    inv = 1.0 / math.sqrt(DK)
    cache_keys = self_cache[:, :, 0].reshape(seq_dev, cache_len, head_count, DK)
    cache_values = self_cache[:, :, 1].reshape(seq_dev, cache_len, head_count, DK)
    s_cache = jnp.einsum(
        "tnhd,nlhd->tnhl", query, cache_keys, preferred_element_type=jnp.float32
    ) * inv
    w_cache = jnp.where(
        cache_usable[None, :, None, :], score_weight(s_cache), jnp.zeros((), jnp.bfloat16)
    )
    s_new = jnp.einsum(
        "tnhd,unhd->tnhu", query, key_new, preferred_element_type=jnp.float32
    ) * inv
    step_at = jnp.arange(steps, dtype=jnp.int32)
    new_usable = step_at[None, :] <= step_at[:, None]
    w_new = jnp.where(
        new_usable[:, None, None, :], score_weight(s_new), jnp.zeros((), jnp.bfloat16)
    )
    weighted = jnp.einsum(
        "tnhl,nlhd->tnhd", w_cache, cache_values, preferred_element_type=jnp.float32
    ) + jnp.einsum("tnhu,unhd->tnhd", w_new, value_new, preferred_element_type=jnp.float32)
    totals = jnp.sum(w_cache.astype(jnp.float32), axis=-1) + jnp.sum(
        w_new.astype(jnp.float32), axis=-1
    )
    context = (weighted / totals[..., None]).reshape(steps, seq_dev, width).astype(jnp.bfloat16)
    context, src_late = lax.optimization_barrier((context, src_pool))
    cross_kv = exchange_sources(
        src_late, assign, my_sources, block_at, enc_at, dp_at, dp_count, enc_count, seq_dev
    )
    context_all = rows_gather(context)
    residual = current + tensor_sum(
        jnp.einsum("tsw,wf->tsf", context_all, w_out_self, preferred_element_type=jnp.float32)
    )

    scaled = (residual * gain_cross[None, None, :]).astype(jnp.bfloat16)
    cq = jnp.einsum("tsd,dw->tsw", scaled, w_q_cross, preferred_element_type=jnp.float32)
    own = rows_reduce_scatter(with_sumsq(cq, residual), seq_dev)
    cross_query = split_norm(own, width).reshape(steps, seq_dev, head_count, DK)
    cross_keys = cross_kv[:, :, 0].reshape(seq_dev, source_len, head_count, DK)
    cross_values = cross_kv[:, :, 1].reshape(seq_dev, source_len, head_count, DK)
    s_cross = jnp.einsum(
        "tnhd,nlhd->tnhl", cross_query, cross_keys, preferred_element_type=jnp.float32
    ) * inv
    w_cross = jnp.where(
        cross_usable[None, :, None, :], score_weight(s_cross), jnp.zeros((), jnp.bfloat16)
    )
    weighted = jnp.einsum(
        "tnhl,nlhd->tnhd", w_cross, cross_values, preferred_element_type=jnp.float32
    )
    totals = jnp.sum(w_cross.astype(jnp.float32), axis=-1)
    context = (weighted / totals[..., None]).reshape(steps, seq_dev, width).astype(jnp.bfloat16)
    context_all = rows_gather(context)
    output_rows = residual + tensor_sum(
        jnp.einsum("tsw,wf->tsf", context_all, w_out_cross, preferred_element_type=jnp.float32)
    )
    return output_rows.astype(jnp.bfloat16)


def solution(mesh):
    in_specs = (
        P(None, "dp", "enc"),
        P(("dp", "enc"), None, None, "tensor"),
        P(("dp", "enc"), None, None, "tensor"),
        P(),
        P(),
        P(),
        P("enc"),
        P("enc", None, "tensor"),
        P("tensor", "enc"),
        P("enc"),
        P("enc", "tensor"),
        P("tensor", "enc"),
    )
    out_specs = P(None, "dp", "enc")
    return jax.shard_map(
        on_device, mesh=mesh, in_specs=in_specs, out_specs=out_specs, check_vma=False
    )
```

```python
import math

import jax
import jax.numpy as jnp
from jax import lax
from jax.sharding import PartitionSpec as P

D = 4096
DK = 256


EPSILON = 1e-06
LANE = 128


def score_weight(scores):
    return jnp.exp(scores).astype(jnp.bfloat16)


def rows_gather(chunk):
    n_enc = lax.axis_size("enc")
    steps, owned, width = chunk.shape
    send = jnp.broadcast_to(chunk[None], (n_enc, steps, owned, width))
    got = lax.all_to_all(send, "enc", 0, 0, tiled=True)
    return got.transpose(1, 0, 2, 3).reshape(steps, n_enc * owned, width)


def tensor_sum(value):
    n_t = lax.axis_size("tensor")
    value = value.astype(jnp.bfloat16)
    terms = [value] + [
        lax.ppermute(value, "tensor", [(i, i ^ k) for i in range(n_t)]) for k in range(1, n_t)
    ]
    terms = [term.astype(jnp.float32) for term in terms]
    while len(terms) > 1:
        terms = [terms[k] + terms[k + 1] for k in range(0, len(terms), 2)]
    return terms[0]


def with_sumsq(partial, rows_in):
    squares = jnp.sum(rows_in * rows_in, axis=-1, keepdims=True)
    high = squares.astype(jnp.bfloat16)
    low = jnp.where(
        jnp.isfinite(squares), squares - high.astype(jnp.float32), 0.0
    ).astype(jnp.bfloat16)
    pad = jnp.zeros(rows_in.shape[:-1] + (LANE - 2,), jnp.bfloat16)
    return jnp.concatenate([partial.astype(jnp.bfloat16), high, low, pad], axis=-1)


def rows_reduce_scatter(partial, owned):
    n_enc = lax.axis_size("enc")
    steps, rows, cols = partial.shape
    send = partial.reshape(steps, n_enc, owned, cols).transpose(1, 0, 2, 3)
    got = lax.all_to_all(send, "enc", 0, 0, tiled=True)
    return jnp.sum(got.astype(jnp.float32), axis=0)


def split_norm(packed, width):
    squares = packed[..., width] + packed[..., width + 1]
    scale = lax.rsqrt(squares / D + EPSILON)
    return (packed[..., :width] * scale[..., None]).astype(jnp.bfloat16)


def exchange_sources(src_pool, assign, my_sources, block_at, enc_at, dp_at, dp_count, enc_count, seq_dev):
    assert seq_dev == dp_count
    my_block = block_at
    source_block = my_sources // seq_dev
    source_row = my_sources % seq_dev
    received = []
    for shift in range(dp_count):
        if shift == 0:
            wanted = my_sources
        else:
            target = (dp_at + shift) % dp_count
            wanted = lax.dynamic_slice_in_dim(
                assign, (target * enc_count + enc_at) * seq_dev, seq_dev
            )
        hit = (wanted // seq_dev) == my_block
        row = jnp.sum(jnp.where(hit, wanted % seq_dev, 0))
        piece = lax.dynamic_index_in_dim(src_pool, row, axis=0, keepdims=False)
        if shift:
            piece = lax.ppermute(
                piece, "dp", [(i, (i + shift) % dp_count) for i in range(dp_count)]
            )
        received.append(piece)
    sender_block = [
        ((dp_at - shift) % dp_count) * enc_count + enc_at for shift in range(dp_count)
    ]
    cross_kv = received[0][None]
    cross_kv = jnp.broadcast_to(cross_kv, (seq_dev,) + cross_kv.shape[1:])
    for shift in range(1, dp_count):
        cross_kv = jnp.where(
            (source_block == sender_block[shift])[:, None, None, None],
            received[shift][None],
            cross_kv,
        )
    return cross_kv


def on_device(
    hidden_in,
    self_cache,
    src_pool,
    assign,
    src_len,
    positions,
    gain_self,
    w_qkv,
    w_out_self,
    gain_cross,
    w_q_cross,
    w_out_cross,
):
    dp_count = lax.axis_size("dp")
    enc_count = lax.axis_size("enc")
    seq_dev = self_cache.shape[0]
    per_pair = seq_dev // dp_count
    cache_len = self_cache.shape[1]
    source_len = src_pool.shape[1]
    width = self_cache.shape[3]
    head_count = width // DK
    steps = hidden_in.shape[0]
    enc_at = lax.axis_index("enc")
    dp_at = lax.axis_index("dp")
    block_at = dp_at * enc_count + enc_at
    slot_index = jnp.arange(seq_dev, dtype=jnp.int32)
    my_slots = block_at * seq_dev + slot_index
    my_positions = lax.dynamic_slice_in_dim(positions, block_at * seq_dev, seq_dev)
    my_sources = lax.dynamic_slice_in_dim(assign, block_at * seq_dev, seq_dev)
    place_at = jnp.arange(cache_len, dtype=jnp.int32)
    cache_usable = place_at[None, :] < my_positions[:, None]
    token_at = jnp.arange(source_len, dtype=jnp.int32)
    source_at = jnp.arange(src_len.shape[0], dtype=jnp.int32)
    my_len = jnp.sum(
        jnp.where(source_at[None, :] == my_sources[:, None], src_len[None, :], 0), axis=1
    )
    cross_usable = token_at[None, :] < my_len[:, None]

    current = hidden_in.astype(jnp.float32)
    scaled = (current * gain_self[None, None, :]).astype(jnp.bfloat16)
    proj = jnp.concatenate(
        [
            jnp.einsum("tsd,dw->tsw", scaled, w_qkv[:, part], preferred_element_type=jnp.float32)
            for part in range(3)
        ],
        axis=-1,
    )
    own = rows_reduce_scatter(with_sumsq(proj, current), seq_dev)
    qkv = split_norm(own, 3 * width).reshape(steps, seq_dev, 3, head_count, DK)
    query = qkv[:, :, 0]
    key_new = qkv[:, :, 1]
    value_new = qkv[:, :, 2]

    inv = 1.0 / math.sqrt(DK)
    cache_keys = self_cache[:, :, 0].reshape(seq_dev, cache_len, head_count, DK)
    cache_values = self_cache[:, :, 1].reshape(seq_dev, cache_len, head_count, DK)
    s_cache = jnp.einsum(
        "tnhd,nlhd->tnhl", query, cache_keys, preferred_element_type=jnp.float32
    ) * inv
    w_cache = jnp.where(
        cache_usable[None, :, None, :], score_weight(s_cache), jnp.zeros((), jnp.bfloat16)
    )
    s_new = jnp.einsum(
        "tnhd,unhd->tnhu", query, key_new, preferred_element_type=jnp.float32
    ) * inv
    step_at = jnp.arange(steps, dtype=jnp.int32)
    new_usable = step_at[None, :] <= step_at[:, None]
    w_new = jnp.where(
        new_usable[:, None, None, :], score_weight(s_new), jnp.zeros((), jnp.bfloat16)
    )
    weighted = jnp.einsum(
        "tnhl,nlhd->tnhd", w_cache, cache_values, preferred_element_type=jnp.float32
    ) + jnp.einsum("tnhu,unhd->tnhd", w_new, value_new, preferred_element_type=jnp.float32)
    totals = jnp.sum(w_cache.astype(jnp.float32), axis=-1) + jnp.sum(
        w_new.astype(jnp.float32), axis=-1
    )
    context = (weighted / totals[..., None]).reshape(steps, seq_dev, width).astype(jnp.bfloat16)
    context, src_late = lax.optimization_barrier((context, src_pool))
    cross_kv = exchange_sources(
        src_late, assign, my_sources, block_at, enc_at, dp_at, dp_count, enc_count, seq_dev
    )
    context_all = rows_gather(context)
    residual = current + tensor_sum(
        jnp.einsum("tsw,wf->tsf", context_all, w_out_self, preferred_element_type=jnp.float32)
    )

    scaled = (residual * gain_cross[None, None, :]).astype(jnp.bfloat16)
    cq = jnp.einsum("tsd,dw->tsw", scaled, w_q_cross, preferred_element_type=jnp.float32)
    own = rows_reduce_scatter(with_sumsq(cq, residual), seq_dev)
    cross_query = split_norm(own, width).reshape(steps, seq_dev, head_count, DK)
    cross_keys = cross_kv[:, :, 0].reshape(seq_dev, source_len, head_count, DK)
    cross_values = cross_kv[:, :, 1].reshape(seq_dev, source_len, head_count, DK)
    s_cross = jnp.einsum(
        "tnhd,nlhd->tnhl", cross_query, cross_keys, preferred_element_type=jnp.float32
    ) * inv
    w_cross = jnp.where(
        cross_usable[None, :, None, :], score_weight(s_cross), jnp.zeros((), jnp.bfloat16)
    )
    weighted = jnp.einsum(
        "tnhl,nlhd->tnhd", w_cross, cross_values, preferred_element_type=jnp.float32
    )
    totals = jnp.sum(w_cross.astype(jnp.float32), axis=-1)
    context = (weighted / totals[..., None]).reshape(steps, seq_dev, width).astype(jnp.bfloat16)
    context_all = rows_gather(context)
    output_rows = residual + tensor_sum(
        jnp.einsum("tsw,wf->tsf", context_all, w_out_cross, preferred_element_type=jnp.float32)
    )
    return output_rows.astype(jnp.bfloat16)


def solution(mesh):
    in_specs = (
        P(None, "dp", "enc"),
        P(("dp", "enc"), None, None, "tensor"),
        P(("dp", "enc"), None, None, "tensor"),
        P(),
        P(),
        P(),
        P("enc"),
        P("enc", None, "tensor"),
        P("tensor", "enc"),
        P("enc"),
        P("enc", "tensor"),
        P("tensor", "enc"),
    )
    out_specs = P(None, "dp", "enc")
    return jax.shard_map(
        on_device, mesh=mesh, in_specs=in_specs, out_specs=out_specs, check_vma=False
    )
```

```python
import math

import jax
import jax.numpy as jnp
from jax import lax
from jax.sharding import PartitionSpec as P

D = 4096
DK = 256


EPSILON = 1e-06
LANE = 128


def score_weight(scores):
    return jnp.exp(scores).astype(jnp.bfloat16)


def rows_gather(chunk):
    n_enc = lax.axis_size("enc")
    steps, owned, width = chunk.shape
    send = jnp.broadcast_to(chunk[None], (n_enc, steps, owned, width))
    got = lax.all_to_all(send, "enc", 0, 0, tiled=True)
    return got.transpose(1, 0, 2, 3).reshape(steps, n_enc * owned, width)


def tensor_sum(value):
    n_t = lax.axis_size("tensor")
    value = value.astype(jnp.bfloat16)
    terms = [value] + [
        lax.ppermute(value, "tensor", [(i, i ^ k) for i in range(n_t)]) for k in range(1, n_t)
    ]
    terms = [term.astype(jnp.float32) for term in terms]
    while len(terms) > 1:
        terms = [terms[k] + terms[k + 1] for k in range(0, len(terms), 2)]
    return terms[0]


def with_sumsq(partial, rows_in):
    squares = jnp.sum(rows_in * rows_in, axis=-1, keepdims=True)
    high = squares.astype(jnp.bfloat16)
    low = jnp.where(
        jnp.isfinite(squares), squares - high.astype(jnp.float32), 0.0
    ).astype(jnp.bfloat16)
    pad = jnp.zeros(rows_in.shape[:-1] + (LANE - 2,), jnp.bfloat16)
    return jnp.concatenate([partial.astype(jnp.bfloat16), high, low, pad], axis=-1)


def rows_reduce_scatter(partial, owned):
    n_enc = lax.axis_size("enc")
    steps, rows, cols = partial.shape
    send = partial.reshape(steps, n_enc, owned, cols).transpose(1, 0, 2, 3)
    got = lax.all_to_all(send, "enc", 0, 0, tiled=True)
    return jnp.sum(got.astype(jnp.float32), axis=0)


def split_norm(packed, width):
    squares = packed[..., width] + packed[..., width + 1]
    scale = lax.rsqrt(squares / D + EPSILON)
    return (packed[..., :width] * scale[..., None]).astype(jnp.bfloat16)


def exchange_sources(src_pool, assign, my_sources, block_at, enc_at, dp_at, dp_count, enc_count, seq_dev):
    assert seq_dev == dp_count
    my_block = block_at
    source_block = my_sources // seq_dev
    source_row = my_sources % seq_dev
    received = []
    for shift in range(dp_count):
        if shift == 0:
            wanted = my_sources
        else:
            target = (dp_at + shift) % dp_count
            wanted = lax.dynamic_slice_in_dim(
                assign, (target * enc_count + enc_at) * seq_dev, seq_dev
            )
        hit = (wanted // seq_dev) == my_block
        row = jnp.sum(jnp.where(hit, wanted % seq_dev, 0))
        piece = lax.dynamic_index_in_dim(src_pool, row, axis=0, keepdims=False)
        if shift:
            piece = lax.ppermute(
                piece, "dp", [(i, (i + shift) % dp_count) for i in range(dp_count)]
            )
        received.append(piece)
    sender_block = [
        ((dp_at - shift) % dp_count) * enc_count + enc_at for shift in range(dp_count)
    ]
    cross_kv = received[0][None]
    cross_kv = jnp.broadcast_to(cross_kv, (seq_dev,) + cross_kv.shape[1:])
    for shift in range(1, dp_count):
        cross_kv = jnp.where(
            (source_block == sender_block[shift])[:, None, None, None],
            received[shift][None],
            cross_kv,
        )
    return cross_kv


def on_device(
    hidden_in,
    self_cache,
    src_pool,
    assign,
    src_len,
    positions,
    gain_self,
    w_qkv,
    w_out_self,
    gain_cross,
    w_q_cross,
    w_out_cross,
):
    dp_count = lax.axis_size("dp")
    enc_count = lax.axis_size("enc")
    seq_dev = self_cache.shape[0]
    per_pair = seq_dev // dp_count
    cache_len = self_cache.shape[1]
    source_len = src_pool.shape[1]
    width = self_cache.shape[3]
    head_count = width // DK
    steps = hidden_in.shape[0]
    enc_at = lax.axis_index("enc")
    dp_at = lax.axis_index("dp")
    block_at = dp_at * enc_count + enc_at
    slot_index = jnp.arange(seq_dev, dtype=jnp.int32)
    my_slots = block_at * seq_dev + slot_index
    my_positions = lax.dynamic_slice_in_dim(positions, block_at * seq_dev, seq_dev)
    my_sources = lax.dynamic_slice_in_dim(assign, block_at * seq_dev, seq_dev)
    place_at = jnp.arange(cache_len, dtype=jnp.int32)
    cache_usable = place_at[None, :] < my_positions[:, None]
    token_at = jnp.arange(source_len, dtype=jnp.int32)
    source_at = jnp.arange(src_len.shape[0], dtype=jnp.int32)
    my_len = jnp.sum(
        jnp.where(source_at[None, :] == my_sources[:, None], src_len[None, :], 0), axis=1
    )
    cross_usable = token_at[None, :] < my_len[:, None]

    current = hidden_in.astype(jnp.float32)
    scaled = (current * gain_self[None, None, :]).astype(jnp.bfloat16)
    proj = jnp.einsum(
        "tsd,dw->tsw",
        scaled,
        w_qkv.reshape(w_qkv.shape[0], 3 * width),
        preferred_element_type=jnp.float32,
    )
    own = rows_reduce_scatter(with_sumsq(proj, current), seq_dev)
    qkv = split_norm(own, 3 * width).reshape(steps, seq_dev, 3, head_count, DK)
    query = qkv[:, :, 0]
    key_new = qkv[:, :, 1]
    value_new = qkv[:, :, 2]

    inv = 1.0 / math.sqrt(DK)
    cache_keys = self_cache[:, :, 0].reshape(seq_dev, cache_len, head_count, DK)
    cache_values = self_cache[:, :, 1].reshape(seq_dev, cache_len, head_count, DK)
    s_cache = jnp.einsum(
        "tnhd,nlhd->tnhl", query, cache_keys, preferred_element_type=jnp.float32
    ) * inv
    w_cache = jnp.where(
        cache_usable[None, :, None, :], score_weight(s_cache), jnp.zeros((), jnp.bfloat16)
    )
    s_new = jnp.einsum(
        "tnhd,unhd->tnhu", query, key_new, preferred_element_type=jnp.float32
    ) * inv
    step_at = jnp.arange(steps, dtype=jnp.int32)
    new_usable = step_at[None, :] <= step_at[:, None]
    w_new = jnp.where(
        new_usable[:, None, None, :], score_weight(s_new), jnp.zeros((), jnp.bfloat16)
    )
    weighted = jnp.einsum(
        "tnhl,nlhd->tnhd", w_cache, cache_values, preferred_element_type=jnp.float32
    ) + jnp.einsum("tnhu,unhd->tnhd", w_new, value_new, preferred_element_type=jnp.float32)
    totals = jnp.sum(w_cache.astype(jnp.float32), axis=-1) + jnp.sum(
        w_new.astype(jnp.float32), axis=-1
    )
    context = (weighted / totals[..., None]).reshape(steps, seq_dev, width).astype(jnp.bfloat16)
    context, src_late = lax.optimization_barrier((context, src_pool))
    cross_kv = exchange_sources(
        src_late, assign, my_sources, block_at, enc_at, dp_at, dp_count, enc_count, seq_dev
    )
    context_all = rows_gather(context)
    residual = current + tensor_sum(
        jnp.einsum("tsw,wf->tsf", context_all, w_out_self, preferred_element_type=jnp.float32)
    )

    scaled = (residual * gain_cross[None, None, :]).astype(jnp.bfloat16)
    cq = jnp.einsum("tsd,dw->tsw", scaled, w_q_cross, preferred_element_type=jnp.float32)
    own = rows_reduce_scatter(with_sumsq(cq, residual), seq_dev)
    cross_query = split_norm(own, width).reshape(steps, seq_dev, head_count, DK)
    cross_keys = cross_kv[:, :, 0].reshape(seq_dev, source_len, head_count, DK)
    cross_values = cross_kv[:, :, 1].reshape(seq_dev, source_len, head_count, DK)
    s_cross = jnp.einsum(
        "tnhd,nlhd->tnhl", cross_query, cross_keys, preferred_element_type=jnp.float32
    ) * inv
    w_cross = jnp.where(
        cross_usable[None, :, None, :], score_weight(s_cross), jnp.zeros((), jnp.bfloat16)
    )
    weighted = jnp.einsum(
        "tnhl,nlhd->tnhd", w_cross, cross_values, preferred_element_type=jnp.float32
    )
    totals = jnp.sum(w_cross.astype(jnp.float32), axis=-1)
    context = (weighted / totals[..., None]).reshape(steps, seq_dev, width).astype(jnp.bfloat16)
    context_all = rows_gather(context)
    output_rows = residual + tensor_sum(
        jnp.einsum("tsw,wf->tsf", context_all, w_out_cross, preferred_element_type=jnp.float32)
    )
    return output_rows.astype(jnp.bfloat16)


def solution(mesh):
    in_specs = (
        P(None, "dp", "enc"),
        P(("dp", "enc"), None, None, "tensor"),
        P(("dp", "enc"), None, None, "tensor"),
        P(),
        P(),
        P(),
        P("enc"),
        P("enc", None, "tensor"),
        P("tensor", "enc"),
        P("enc"),
        P("enc", "tensor"),
        P("tensor", "enc"),
    )
    out_specs = P(None, "dp", "enc")
    return jax.shard_map(
        on_device, mesh=mesh, in_specs=in_specs, out_specs=out_specs, check_vma=False
    )
```

```python
import math

import jax
import jax.numpy as jnp
from jax import lax
from jax.sharding import PartitionSpec as P

D = 4096
DK = 256


EPSILON = 1e-06
LANE = 128


def score_weight(scores):
    return jnp.exp(scores).astype(jnp.bfloat16)


def rows_gather(chunk):
    n_enc = lax.axis_size("enc")
    steps, owned, width = chunk.shape
    send = jnp.broadcast_to(chunk[None], (n_enc, steps, owned, width))
    got = lax.all_to_all(send, "enc", 0, 0, tiled=True)
    return got.transpose(1, 0, 2, 3).reshape(steps, n_enc * owned, width)


def tensor_sum(value):
    n_t = lax.axis_size("tensor")
    value = value.astype(jnp.bfloat16)
    terms = [value] + [
        lax.ppermute(value, "tensor", [(i, i ^ k) for i in range(n_t)]) for k in range(1, n_t)
    ]
    terms = [term.astype(jnp.float32) for term in terms]
    while len(terms) > 1:
        terms = [terms[k] + terms[k + 1] for k in range(0, len(terms), 2)]
    return terms[0]


def with_sumsq(partial, rows_in):
    squares = jnp.sum(rows_in * rows_in, axis=-1, keepdims=True)
    high = squares.astype(jnp.bfloat16)
    low = jnp.where(
        jnp.isfinite(squares), squares - high.astype(jnp.float32), 0.0
    ).astype(jnp.bfloat16)
    pad = jnp.zeros(rows_in.shape[:-1] + (LANE - 2,), jnp.bfloat16)
    return jnp.concatenate([partial.astype(jnp.bfloat16), high, low, pad], axis=-1)


def rows_reduce_scatter(partial, owned):
    n_enc = lax.axis_size("enc")
    steps, rows, cols = partial.shape
    send = partial.reshape(steps, n_enc, owned, cols).transpose(1, 0, 2, 3)
    got = lax.all_to_all(send, "enc", 0, 0, tiled=True)
    return jnp.sum(got.astype(jnp.float32), axis=0)


def split_norm(packed, width):
    squares = packed[..., width] + packed[..., width + 1]
    scale = lax.rsqrt(squares / D + EPSILON)
    return (packed[..., :width] * scale[..., None]).astype(jnp.bfloat16)


def exchange_sources(src_pool, assign, my_sources, block_at, enc_at, dp_at, dp_count, enc_count, seq_dev):
    assert seq_dev == dp_count
    my_block = block_at
    source_block = my_sources // seq_dev
    source_row = my_sources % seq_dev
    received = []
    for shift in range(dp_count):
        if shift == 0:
            wanted = my_sources
        else:
            target = (dp_at + shift) % dp_count
            wanted = lax.dynamic_slice_in_dim(
                assign, (target * enc_count + enc_at) * seq_dev, seq_dev
            )
        hit = (wanted // seq_dev) == my_block
        row = jnp.sum(jnp.where(hit, wanted % seq_dev, 0))
        piece = lax.dynamic_index_in_dim(src_pool, row, axis=0, keepdims=False)
        if shift:
            piece = lax.ppermute(
                piece, "dp", [(i, (i + shift) % dp_count) for i in range(dp_count)]
            )
        received.append(piece)
    sender_block = [
        ((dp_at - shift) % dp_count) * enc_count + enc_at for shift in range(dp_count)
    ]
    cross_kv = received[0][None]
    cross_kv = jnp.broadcast_to(cross_kv, (seq_dev,) + cross_kv.shape[1:])
    for shift in range(1, dp_count):
        cross_kv = jnp.where(
            (source_block == sender_block[shift])[:, None, None, None],
            received[shift][None],
            cross_kv,
        )
    return cross_kv


def on_device(
    hidden_in,
    self_cache,
    src_pool,
    assign,
    src_len,
    positions,
    gain_self,
    w_qkv,
    w_out_self,
    gain_cross,
    w_q_cross,
    w_out_cross,
):
    dp_count = lax.axis_size("dp")
    enc_count = lax.axis_size("enc")
    seq_dev = self_cache.shape[0]
    per_pair = seq_dev // dp_count
    cache_len = self_cache.shape[1]
    source_len = src_pool.shape[1]
    width = self_cache.shape[3]
    head_count = width // DK
    steps = hidden_in.shape[0]
    enc_at = lax.axis_index("enc")
    dp_at = lax.axis_index("dp")
    block_at = dp_at * enc_count + enc_at
    slot_index = jnp.arange(seq_dev, dtype=jnp.int32)
    my_slots = block_at * seq_dev + slot_index
    my_positions = lax.dynamic_slice_in_dim(positions, block_at * seq_dev, seq_dev)
    my_sources = lax.dynamic_slice_in_dim(assign, block_at * seq_dev, seq_dev)
    place_at = jnp.arange(cache_len, dtype=jnp.int32)
    cache_usable = place_at[None, :] < my_positions[:, None]
    token_at = jnp.arange(source_len, dtype=jnp.int32)
    source_at = jnp.arange(src_len.shape[0], dtype=jnp.int32)
    my_len = jnp.sum(
        jnp.where(source_at[None, :] == my_sources[:, None], src_len[None, :], 0), axis=1
    )
    cross_usable = token_at[None, :] < my_len[:, None]

    current = hidden_in.astype(jnp.float32)
    scaled = (current * gain_self[None, None, :]).astype(jnp.bfloat16)
    proj = jnp.einsum("tsd,dcw->tscw", scaled, w_qkv, preferred_element_type=jnp.float32)
    proj = proj.reshape(steps, current.shape[1], 3 * width)
    own = rows_reduce_scatter(with_sumsq(proj, current), seq_dev)
    qkv = split_norm(own, 3 * width).reshape(steps, seq_dev, 3, head_count, DK)
    query = qkv[:, :, 0]
    key_new = qkv[:, :, 1]
    value_new = qkv[:, :, 2]

    inv = 1.0 / math.sqrt(DK)
    cache_keys = self_cache[:, :, 0].reshape(seq_dev, cache_len, head_count, DK)
    cache_values = self_cache[:, :, 1].reshape(seq_dev, cache_len, head_count, DK)
    s_cache = jnp.einsum(
        "tnhd,nlhd->tnhl", query, cache_keys, preferred_element_type=jnp.float32
    ) * inv
    w_cache = jnp.where(
        cache_usable[None, :, None, :], score_weight(s_cache), jnp.zeros((), jnp.bfloat16)
    )
    s_new = jnp.einsum(
        "tnhd,unhd->tnhu", query, key_new, preferred_element_type=jnp.float32
    ) * inv
    step_at = jnp.arange(steps, dtype=jnp.int32)
    new_usable = step_at[None, :] <= step_at[:, None]
    w_new = jnp.where(
        new_usable[:, None, None, :], score_weight(s_new), jnp.zeros((), jnp.bfloat16)
    )
    weighted = jnp.einsum(
        "tnhl,nlhd->tnhd", w_cache, cache_values, preferred_element_type=jnp.float32
    ) + jnp.einsum("tnhu,unhd->tnhd", w_new, value_new, preferred_element_type=jnp.float32)
    totals = jnp.sum(w_cache.astype(jnp.float32), axis=-1) + jnp.sum(
        w_new.astype(jnp.float32), axis=-1
    )
    context = (weighted / totals[..., None]).reshape(steps, seq_dev, width).astype(jnp.bfloat16)
    context_all = rows_gather(context)
    partial_out = jnp.einsum(
        "tsw,wf->tsf", context_all, w_out_self, preferred_element_type=jnp.float32
    )
    partial_out, src_late = lax.optimization_barrier((partial_out, src_pool))
    cross_kv = exchange_sources(
        src_late, assign, my_sources, block_at, enc_at, dp_at, dp_count, enc_count, seq_dev
    )
    residual = current + tensor_sum(partial_out)

    scaled = (residual * gain_cross[None, None, :]).astype(jnp.bfloat16)
    cq = jnp.einsum("tsd,dw->tsw", scaled, w_q_cross, preferred_element_type=jnp.float32)
    own = rows_reduce_scatter(with_sumsq(cq, residual), seq_dev)
    cross_query = split_norm(own, width).reshape(steps, seq_dev, head_count, DK)
    cross_keys = cross_kv[:, :, 0].reshape(seq_dev, source_len, head_count, DK)
    cross_values = cross_kv[:, :, 1].reshape(seq_dev, source_len, head_count, DK)
    s_cross = jnp.einsum(
        "tnhd,nlhd->tnhl", cross_query, cross_keys, preferred_element_type=jnp.float32
    ) * inv
    w_cross = jnp.where(
        cross_usable[None, :, None, :], score_weight(s_cross), jnp.zeros((), jnp.bfloat16)
    )
    weighted = jnp.einsum(
        "tnhl,nlhd->tnhd", w_cross, cross_values, preferred_element_type=jnp.float32
    )
    totals = jnp.sum(w_cross.astype(jnp.float32), axis=-1)
    context = (weighted / totals[..., None]).reshape(steps, seq_dev, width).astype(jnp.bfloat16)
    context_all = rows_gather(context)
    output_rows = residual + tensor_sum(
        jnp.einsum("tsw,wf->tsf", context_all, w_out_cross, preferred_element_type=jnp.float32)
    )
    return output_rows.astype(jnp.bfloat16)


def solution(mesh):
    in_specs = (
        P(None, "dp", "enc"),
        P(("dp", "enc"), None, None, "tensor"),
        P(("dp", "enc"), None, None, "tensor"),
        P(),
        P(),
        P(),
        P("enc"),
        P("enc", None, "tensor"),
        P("tensor", "enc"),
        P("enc"),
        P("enc", "tensor"),
        P("tensor", "enc"),
    )
    out_specs = P(None, "dp", "enc")
    return jax.shard_map(
        on_device, mesh=mesh, in_specs=in_specs, out_specs=out_specs, check_vma=False
    )
```

```python
import math

import jax
import jax.numpy as jnp
from jax import lax
from jax.sharding import PartitionSpec as P

D = 4096
DK = 256


EPSILON = 1e-06
LANE = 128


def score_weight(scores):
    return jnp.exp(scores).astype(jnp.bfloat16)


def rows_gather(chunk):
    n_enc = lax.axis_size("enc")
    steps, owned, width = chunk.shape
    send = jnp.broadcast_to(chunk[None], (n_enc, steps, owned, width))
    got = lax.all_to_all(send, "enc", 0, 0, tiled=True)
    return got.transpose(1, 0, 2, 3).reshape(steps, n_enc * owned, width)


def tensor_sum(value):
    n_t = lax.axis_size("tensor")
    value = value.astype(jnp.bfloat16)
    terms = [value] + [
        lax.ppermute(value, "tensor", [(i, i ^ k) for i in range(n_t)]) for k in range(1, n_t)
    ]
    terms = [term.astype(jnp.float32) for term in terms]
    while len(terms) > 1:
        terms = [terms[k] + terms[k + 1] for k in range(0, len(terms), 2)]
    return terms[0]


def with_sumsq(partial, rows_in):
    squares = jnp.sum(rows_in * rows_in, axis=-1, keepdims=True)
    high = squares.astype(jnp.bfloat16)
    low = jnp.where(
        jnp.isfinite(squares), squares - high.astype(jnp.float32), 0.0
    ).astype(jnp.bfloat16)
    pad = jnp.zeros(rows_in.shape[:-1] + (LANE - 2,), jnp.bfloat16)
    return jnp.concatenate([partial.astype(jnp.bfloat16), high, low, pad], axis=-1)


def rows_reduce_scatter(partial, owned):
    n_enc = lax.axis_size("enc")
    steps, rows, cols = partial.shape
    send = partial.reshape(steps, n_enc, owned, cols).transpose(1, 0, 2, 3)
    got = lax.all_to_all(send, "enc", 0, 0, tiled=True)
    return jnp.sum(got.astype(jnp.float32), axis=0)


def split_norm(packed, width):
    squares = packed[..., width] + packed[..., width + 1]
    scale = lax.rsqrt(squares / D + EPSILON)
    return (packed[..., :width] * scale[..., None]).astype(jnp.bfloat16)


def exchange_sources(src_pool, assign, my_sources, block_at, enc_at, dp_at, dp_count, enc_count, seq_dev):
    assert seq_dev == dp_count
    my_block = block_at
    source_block = my_sources // seq_dev
    source_row = my_sources % seq_dev
    received = []
    for shift in range(dp_count):
        if shift == 0:
            wanted = my_sources
        else:
            target = (dp_at + shift) % dp_count
            wanted = lax.dynamic_slice_in_dim(
                assign, (target * enc_count + enc_at) * seq_dev, seq_dev
            )
        hit = (wanted // seq_dev) == my_block
        row = jnp.sum(jnp.where(hit, wanted % seq_dev, 0))
        piece = lax.dynamic_index_in_dim(src_pool, row, axis=0, keepdims=False)
        if shift:
            piece = lax.ppermute(
                piece, "dp", [(i, (i + shift) % dp_count) for i in range(dp_count)]
            )
        received.append(piece)
    sender_block = [
        ((dp_at - shift) % dp_count) * enc_count + enc_at for shift in range(dp_count)
    ]
    cross_kv = received[0][None]
    cross_kv = jnp.broadcast_to(cross_kv, (seq_dev,) + cross_kv.shape[1:])
    for shift in range(1, dp_count):
        cross_kv = jnp.where(
            (source_block == sender_block[shift])[:, None, None, None],
            received[shift][None],
            cross_kv,
        )
    return cross_kv


def on_device(
    hidden_in,
    self_cache,
    src_pool,
    assign,
    src_len,
    positions,
    gain_self,
    w_qkv,
    w_out_self,
    gain_cross,
    w_q_cross,
    w_out_cross,
):
    dp_count = lax.axis_size("dp")
    enc_count = lax.axis_size("enc")
    seq_dev = self_cache.shape[0]
    per_pair = seq_dev // dp_count
    cache_len = self_cache.shape[1]
    source_len = src_pool.shape[1]
    width = self_cache.shape[3]
    head_count = width // DK
    steps = hidden_in.shape[0]
    enc_at = lax.axis_index("enc")
    dp_at = lax.axis_index("dp")
    block_at = dp_at * enc_count + enc_at
    slot_index = jnp.arange(seq_dev, dtype=jnp.int32)
    my_slots = block_at * seq_dev + slot_index
    my_positions = lax.dynamic_slice_in_dim(positions, block_at * seq_dev, seq_dev)
    my_sources = lax.dynamic_slice_in_dim(assign, block_at * seq_dev, seq_dev)
    place_at = jnp.arange(cache_len, dtype=jnp.int32)
    cache_usable = place_at[None, :] < my_positions[:, None]
    token_at = jnp.arange(source_len, dtype=jnp.int32)
    source_at = jnp.arange(src_len.shape[0], dtype=jnp.int32)
    my_len = jnp.sum(
        jnp.where(source_at[None, :] == my_sources[:, None], src_len[None, :], 0), axis=1
    )
    cross_usable = token_at[None, :] < my_len[:, None]

    w_q_gained = (gain_cross[:, None] * w_q_cross.astype(jnp.float32)).astype(jnp.bfloat16)

    current = hidden_in.astype(jnp.float32)
    scaled = (current * gain_self[None, None, :]).astype(jnp.bfloat16)
    proj = jnp.einsum("tsd,dcw->tscw", scaled, w_qkv, preferred_element_type=jnp.float32)
    proj = proj.reshape(steps, current.shape[1], 3 * width)
    own = rows_reduce_scatter(with_sumsq(proj, current), seq_dev)
    qkv = split_norm(own, 3 * width).reshape(steps, seq_dev, 3, head_count, DK)
    query = qkv[:, :, 0]
    key_new = qkv[:, :, 1]
    value_new = qkv[:, :, 2]

    inv = 1.0 / math.sqrt(DK)
    cache_keys = self_cache[:, :, 0].reshape(seq_dev, cache_len, head_count, DK)
    cache_values = self_cache[:, :, 1].reshape(seq_dev, cache_len, head_count, DK)
    s_cache = jnp.einsum(
        "tnhd,nlhd->tnhl", query, cache_keys, preferred_element_type=jnp.float32
    ) * inv
    w_cache = jnp.where(
        cache_usable[None, :, None, :], score_weight(s_cache), jnp.zeros((), jnp.bfloat16)
    )
    s_new = jnp.einsum(
        "tnhd,unhd->tnhu", query, key_new, preferred_element_type=jnp.float32
    ) * inv
    step_at = jnp.arange(steps, dtype=jnp.int32)
    new_usable = step_at[None, :] <= step_at[:, None]
    w_new = jnp.where(
        new_usable[:, None, None, :], score_weight(s_new), jnp.zeros((), jnp.bfloat16)
    )
    weighted = jnp.einsum(
        "tnhl,nlhd->tnhd", w_cache, cache_values, preferred_element_type=jnp.float32
    ) + jnp.einsum("tnhu,unhd->tnhd", w_new, value_new, preferred_element_type=jnp.float32)
    totals = jnp.sum(w_cache.astype(jnp.float32), axis=-1) + jnp.sum(
        w_new.astype(jnp.float32), axis=-1
    )
    context = (weighted / totals[..., None]).reshape(steps, seq_dev, width).astype(jnp.bfloat16)
    context_all = rows_gather(context)
    partial_out = jnp.einsum(
        "tsw,wf->tsf", context_all, w_out_self, preferred_element_type=jnp.float32
    )
    partial_out, src_late, w_q_gained = lax.optimization_barrier(
        (partial_out, src_pool, w_q_gained)
    )
    cross_kv = exchange_sources(
        src_late, assign, my_sources, block_at, enc_at, dp_at, dp_count, enc_count, seq_dev
    )
    residual = current + tensor_sum(partial_out)

    cq = jnp.einsum(
        "tsd,dw->tsw", residual.astype(jnp.bfloat16), w_q_gained, preferred_element_type=jnp.float32
    )
    own = rows_reduce_scatter(with_sumsq(cq, residual), seq_dev)
    cross_query = split_norm(own, width).reshape(steps, seq_dev, head_count, DK)
    cross_keys = cross_kv[:, :, 0].reshape(seq_dev, source_len, head_count, DK)
    cross_values = cross_kv[:, :, 1].reshape(seq_dev, source_len, head_count, DK)
    s_cross = jnp.einsum(
        "tnhd,nlhd->tnhl", cross_query, cross_keys, preferred_element_type=jnp.float32
    ) * inv
    w_cross = jnp.where(
        cross_usable[None, :, None, :], score_weight(s_cross), jnp.zeros((), jnp.bfloat16)
    )
    weighted = jnp.einsum(
        "tnhl,nlhd->tnhd", w_cross, cross_values, preferred_element_type=jnp.float32
    )
    totals = jnp.sum(w_cross.astype(jnp.float32), axis=-1)
    context = (weighted / totals[..., None]).reshape(steps, seq_dev, width).astype(jnp.bfloat16)
    context_all = rows_gather(context)
    output_rows = residual + tensor_sum(
        jnp.einsum("tsw,wf->tsf", context_all, w_out_cross, preferred_element_type=jnp.float32)
    )
    return output_rows.astype(jnp.bfloat16)


def solution(mesh):
    in_specs = (
        P(None, "dp", "enc"),
        P(("dp", "enc"), None, None, "tensor"),
        P(("dp", "enc"), None, None, "tensor"),
        P(),
        P(),
        P(),
        P("enc"),
        P("enc", None, "tensor"),
        P("tensor", "enc"),
        P("enc"),
        P("enc", "tensor"),
        P("tensor", "enc"),
    )
    out_specs = P(None, "dp", "enc")
    return jax.shard_map(
        on_device, mesh=mesh, in_specs=in_specs, out_specs=out_specs, check_vma=False
    )
```

```python
import math

import jax
import jax.numpy as jnp
from jax import lax
from jax.sharding import PartitionSpec as P

D = 4096
DK = 256


EPSILON = 1e-06
LANE = 128


def score_weight(scores):
    return jnp.exp(scores).astype(jnp.bfloat16)


def rows_gather(chunk):
    n_enc = lax.axis_size("enc")
    steps, owned, width = chunk.shape
    send = jnp.broadcast_to(chunk[None], (n_enc, steps, owned, width))
    got = lax.all_to_all(send, "enc", 0, 0, tiled=True)
    return got.transpose(1, 0, 2, 3).reshape(steps, n_enc * owned, width)


def tensor_sum(value):
    n_t = lax.axis_size("tensor")
    value = value.astype(jnp.bfloat16)
    terms = [value] + [
        lax.ppermute(value, "tensor", [(i, i ^ k) for i in range(n_t)]) for k in range(1, n_t)
    ]
    terms = [term.astype(jnp.float32) for term in terms]
    while len(terms) > 1:
        terms = [terms[k] + terms[k + 1] for k in range(0, len(terms), 2)]
    return terms[0]


def with_sumsq(partial, rows_in):
    squares = jnp.sum(rows_in * rows_in, axis=-1, keepdims=True)
    high = squares.astype(jnp.bfloat16)
    low = jnp.where(
        jnp.isfinite(squares), squares - high.astype(jnp.float32), 0.0
    ).astype(jnp.bfloat16)
    pad = jnp.zeros(rows_in.shape[:-1] + (LANE - 2,), jnp.bfloat16)
    return jnp.concatenate([partial.astype(jnp.bfloat16), high, low, pad], axis=-1)


def rows_reduce_scatter(partial, owned):
    n_enc = lax.axis_size("enc")
    steps, rows, cols = partial.shape
    send = partial.reshape(steps, n_enc, owned, cols).transpose(1, 0, 2, 3)
    got = lax.all_to_all(send, "enc", 0, 0, tiled=True)
    return jnp.sum(got.astype(jnp.float32), axis=0)


def split_norm(packed, width):
    squares = packed[..., width] + packed[..., width + 1]
    scale = lax.rsqrt(squares / D + EPSILON)
    return (packed[..., :width] * scale[..., None]).astype(jnp.bfloat16)


def exchange_sources(src_pool, assign, my_sources, block_at, enc_at, dp_at, dp_count, enc_count, seq_dev):
    assert seq_dev == dp_count
    my_block = block_at
    source_block = my_sources // seq_dev
    source_row = my_sources % seq_dev
    received = []
    for shift in range(dp_count):
        if shift == 0:
            wanted = my_sources
        else:
            target = (dp_at + shift) % dp_count
            wanted = lax.dynamic_slice_in_dim(
                assign, (target * enc_count + enc_at) * seq_dev, seq_dev
            )
        hit = (wanted // seq_dev) == my_block
        row = jnp.sum(jnp.where(hit, wanted % seq_dev, 0))
        piece = lax.dynamic_index_in_dim(src_pool, row, axis=0, keepdims=False)
        if shift:
            piece = lax.ppermute(
                piece, "dp", [(i, (i + shift) % dp_count) for i in range(dp_count)]
            )
        received.append(piece)
    sender_block = [
        ((dp_at - shift) % dp_count) * enc_count + enc_at for shift in range(dp_count)
    ]
    cross_kv = received[0][None]
    cross_kv = jnp.broadcast_to(cross_kv, (seq_dev,) + cross_kv.shape[1:])
    for shift in range(1, dp_count):
        cross_kv = jnp.where(
            (source_block == sender_block[shift])[:, None, None, None],
            received[shift][None],
            cross_kv,
        )
    return cross_kv


def on_device(
    hidden_in,
    self_cache,
    src_pool,
    assign,
    src_len,
    positions,
    gain_self,
    w_qkv,
    w_out_self,
    gain_cross,
    w_q_cross,
    w_out_cross,
):
    dp_count = lax.axis_size("dp")
    enc_count = lax.axis_size("enc")
    seq_dev = self_cache.shape[0]
    per_pair = seq_dev // dp_count
    cache_len = self_cache.shape[1]
    source_len = src_pool.shape[1]
    width = self_cache.shape[3]
    head_count = width // DK
    steps = hidden_in.shape[0]
    enc_at = lax.axis_index("enc")
    dp_at = lax.axis_index("dp")
    block_at = dp_at * enc_count + enc_at
    slot_index = jnp.arange(seq_dev, dtype=jnp.int32)
    my_slots = block_at * seq_dev + slot_index
    my_positions = lax.dynamic_slice_in_dim(positions, block_at * seq_dev, seq_dev)
    my_sources = lax.dynamic_slice_in_dim(assign, block_at * seq_dev, seq_dev)
    place_at = jnp.arange(cache_len, dtype=jnp.int32)
    cache_usable = place_at[None, :] < my_positions[:, None]
    token_at = jnp.arange(source_len, dtype=jnp.int32)
    source_at = jnp.arange(src_len.shape[0], dtype=jnp.int32)
    my_len = jnp.sum(
        jnp.where(source_at[None, :] == my_sources[:, None], src_len[None, :], 0), axis=1
    )
    cross_usable = token_at[None, :] < my_len[:, None]

    w_q_gained = (gain_cross[:, None] * w_q_cross.astype(jnp.float32)).astype(jnp.bfloat16)

    current = hidden_in.astype(jnp.float32)
    scaled = (current * gain_self[None, None, :]).astype(jnp.bfloat16)
    proj = jnp.einsum("tsd,dcw->tscw", scaled, w_qkv, preferred_element_type=jnp.float32)
    proj = proj.reshape(steps, current.shape[1], 3 * width)
    own = rows_reduce_scatter(with_sumsq(proj, current), seq_dev)
    qkv = split_norm(own, 3 * width).reshape(steps, seq_dev, 3, head_count, DK)
    query = qkv[:, :, 0]
    key_new = qkv[:, :, 1]
    value_new = qkv[:, :, 2]

    inv = 1.0 / math.sqrt(DK)
    cache_keys = self_cache[:, :, 0].reshape(seq_dev, cache_len, head_count, DK)
    cache_values = self_cache[:, :, 1].reshape(seq_dev, cache_len, head_count, DK)
    s_cache = jnp.einsum(
        "tnhd,nlhd->tnhl", query, cache_keys, preferred_element_type=jnp.float32
    ) * inv
    w_cache = jnp.where(
        cache_usable[None, :, None, :], score_weight(s_cache), jnp.zeros((), jnp.bfloat16)
    )
    s_new = jnp.einsum(
        "tnhd,unhd->tnhu", query, key_new, preferred_element_type=jnp.float32
    ) * inv
    step_at = jnp.arange(steps, dtype=jnp.int32)
    new_usable = step_at[None, :] <= step_at[:, None]
    w_new = jnp.where(
        new_usable[:, None, None, :], score_weight(s_new), jnp.zeros((), jnp.bfloat16)
    )
    weighted = jnp.einsum(
        "tnhl,nlhd->tnhd", w_cache, cache_values, preferred_element_type=jnp.float32
    ) + jnp.einsum("tnhu,unhd->tnhd", w_new, value_new, preferred_element_type=jnp.float32)
    totals = jnp.sum(w_cache.astype(jnp.float32), axis=-1) + jnp.sum(
        w_new.astype(jnp.float32), axis=-1
    )
    context = (weighted / totals[..., None]).reshape(steps, seq_dev, width).astype(jnp.bfloat16)
    context_all = rows_gather(context)
    partial_out = jnp.einsum(
        "tsw,wf->tsf", context_all, w_out_self, preferred_element_type=jnp.float32
    )
    partial_out, w_q_gained = lax.optimization_barrier((partial_out, w_q_gained))
    src_late = src_pool
    cross_kv = exchange_sources(
        src_late, assign, my_sources, block_at, enc_at, dp_at, dp_count, enc_count, seq_dev
    )
    residual = current + tensor_sum(partial_out)

    cq = jnp.einsum(
        "tsd,dw->tsw", residual.astype(jnp.bfloat16), w_q_gained, preferred_element_type=jnp.float32
    )
    own = rows_reduce_scatter(with_sumsq(cq, residual), seq_dev)
    cross_query = split_norm(own, width).reshape(steps, seq_dev, head_count, DK)
    cross_keys = cross_kv[:, :, 0].reshape(seq_dev, source_len, head_count, DK)
    cross_values = cross_kv[:, :, 1].reshape(seq_dev, source_len, head_count, DK)
    s_cross = jnp.einsum(
        "tnhd,nlhd->tnhl", cross_query, cross_keys, preferred_element_type=jnp.float32
    ) * inv
    w_cross = jnp.where(
        cross_usable[None, :, None, :], score_weight(s_cross), jnp.zeros((), jnp.bfloat16)
    )
    weighted = jnp.einsum(
        "tnhl,nlhd->tnhd", w_cross, cross_values, preferred_element_type=jnp.float32
    )
    totals = jnp.sum(w_cross.astype(jnp.float32), axis=-1)
    context = (weighted / totals[..., None]).reshape(steps, seq_dev, width).astype(jnp.bfloat16)
    context_all = rows_gather(context)
    output_rows = residual + tensor_sum(
        jnp.einsum("tsw,wf->tsf", context_all, w_out_cross, preferred_element_type=jnp.float32)
    )
    return output_rows.astype(jnp.bfloat16)


def solution(mesh):
    in_specs = (
        P(None, "dp", "enc"),
        P(("dp", "enc"), None, None, "tensor"),
        P(("dp", "enc"), None, None, "tensor"),
        P(),
        P(),
        P(),
        P("enc"),
        P("enc", None, "tensor"),
        P("tensor", "enc"),
        P("enc"),
        P("enc", "tensor"),
        P("tensor", "enc"),
    )
    out_specs = P(None, "dp", "enc")
    return jax.shard_map(
        on_device, mesh=mesh, in_specs=in_specs, out_specs=out_specs, check_vma=False
    )
```

```python
import math

import jax
import jax.numpy as jnp
from jax import lax
from jax.sharding import PartitionSpec as P

D = 4096
DK = 256


EPSILON = 1e-06
LANE = 128


def score_weight(scores):
    return jnp.exp(scores).astype(jnp.bfloat16)


def rows_gather(chunk):
    n_enc = lax.axis_size("enc")
    steps, owned, width = chunk.shape
    send = jnp.broadcast_to(chunk[None], (n_enc, steps, owned, width))
    got = lax.all_to_all(send, "enc", 0, 0, tiled=True)
    return got.transpose(1, 0, 2, 3).reshape(steps, n_enc * owned, width)


def tensor_sum(value):
    n_t = lax.axis_size("tensor")
    value = value.astype(jnp.bfloat16)
    terms = [value] + [
        lax.ppermute(value, "tensor", [(i, i ^ k) for i in range(n_t)]) for k in range(1, n_t)
    ]
    terms = [term.astype(jnp.float32) for term in terms]
    while len(terms) > 1:
        terms = [terms[k] + terms[k + 1] for k in range(0, len(terms), 2)]
    return terms[0]


def with_sumsq(partial, rows_in):
    squares = jnp.sum(rows_in * rows_in, axis=-1, keepdims=True)
    high = squares.astype(jnp.bfloat16)
    low = jnp.where(
        jnp.isfinite(squares), squares - high.astype(jnp.float32), 0.0
    ).astype(jnp.bfloat16)
    pad = jnp.zeros(rows_in.shape[:-1] + (LANE - 2,), jnp.bfloat16)
    return jnp.concatenate([partial.astype(jnp.bfloat16), high, low, pad], axis=-1)


def rows_reduce_scatter(partial, owned):
    n_enc = lax.axis_size("enc")
    steps, rows, cols = partial.shape
    send = partial.reshape(steps, n_enc, owned, cols).transpose(1, 0, 2, 3)
    got = lax.all_to_all(send, "enc", 0, 0, tiled=True)
    return jnp.sum(got.astype(jnp.float32), axis=0)


def split_norm(packed, width):
    squares = packed[..., width] + packed[..., width + 1]
    scale = lax.rsqrt(squares / D + EPSILON)
    return (packed[..., :width] * scale[..., None]).astype(jnp.bfloat16)


def exchange_sources(src_pool, assign, my_sources, block_at, enc_at, dp_at, dp_count, enc_count, seq_dev):
    assert seq_dev == dp_count
    my_block = block_at
    source_block = my_sources // seq_dev
    source_row = my_sources % seq_dev
    received = []
    for shift in range(dp_count):
        if shift == 0:
            wanted = my_sources
        else:
            target = (dp_at + shift) % dp_count
            wanted = lax.dynamic_slice_in_dim(
                assign, (target * enc_count + enc_at) * seq_dev, seq_dev
            )
        hit = (wanted // seq_dev) == my_block
        row = jnp.sum(jnp.where(hit, wanted % seq_dev, 0))
        piece = lax.dynamic_index_in_dim(src_pool, row, axis=0, keepdims=False)
        if shift:
            piece = lax.ppermute(
                piece, "dp", [(i, (i + shift) % dp_count) for i in range(dp_count)]
            )
        received.append(piece)
    sender_block = [
        ((dp_at - shift) % dp_count) * enc_count + enc_at for shift in range(dp_count)
    ]
    cross_kv = received[0][None]
    cross_kv = jnp.broadcast_to(cross_kv, (seq_dev,) + cross_kv.shape[1:])
    for shift in range(1, dp_count):
        cross_kv = jnp.where(
            (source_block == sender_block[shift])[:, None, None, None],
            received[shift][None],
            cross_kv,
        )
    return cross_kv


def on_device(
    hidden_in,
    self_cache,
    src_pool,
    assign,
    src_len,
    positions,
    gain_self,
    w_qkv,
    w_out_self,
    gain_cross,
    w_q_cross,
    w_out_cross,
):
    dp_count = lax.axis_size("dp")
    enc_count = lax.axis_size("enc")
    seq_dev = self_cache.shape[0]
    per_pair = seq_dev // dp_count
    cache_len = self_cache.shape[1]
    source_len = src_pool.shape[1]
    width = self_cache.shape[3]
    head_count = width // DK
    steps = hidden_in.shape[0]
    enc_at = lax.axis_index("enc")
    dp_at = lax.axis_index("dp")
    block_at = dp_at * enc_count + enc_at
    slot_index = jnp.arange(seq_dev, dtype=jnp.int32)
    my_slots = block_at * seq_dev + slot_index
    my_positions = lax.dynamic_slice_in_dim(positions, block_at * seq_dev, seq_dev)
    my_sources = lax.dynamic_slice_in_dim(assign, block_at * seq_dev, seq_dev)
    place_at = jnp.arange(cache_len, dtype=jnp.int32)
    cache_usable = place_at[None, :] < my_positions[:, None]
    token_at = jnp.arange(source_len, dtype=jnp.int32)
    source_at = jnp.arange(src_len.shape[0], dtype=jnp.int32)
    my_len = jnp.sum(
        jnp.where(source_at[None, :] == my_sources[:, None], src_len[None, :], 0), axis=1
    )
    cross_usable = token_at[None, :] < my_len[:, None]

    w_q_gained = (gain_cross[:, None] * w_q_cross.astype(jnp.float32)).astype(jnp.bfloat16)

    cross_kv = exchange_sources(
        src_pool, assign, my_sources, block_at, enc_at, dp_at, dp_count, enc_count, seq_dev
    )
    cross_kv, hidden_in = lax.optimization_barrier((cross_kv, hidden_in))

    current = hidden_in.astype(jnp.float32)
    scaled = (current * gain_self[None, None, :]).astype(jnp.bfloat16)
    proj = jnp.einsum("tsd,dcw->tscw", scaled, w_qkv, preferred_element_type=jnp.float32)
    proj = proj.reshape(steps, current.shape[1], 3 * width)
    own = rows_reduce_scatter(with_sumsq(proj, current), seq_dev)
    qkv = split_norm(own, 3 * width).reshape(steps, seq_dev, 3, head_count, DK)
    query = qkv[:, :, 0]
    key_new = qkv[:, :, 1]
    value_new = qkv[:, :, 2]

    inv = 1.0 / math.sqrt(DK)
    cache_keys = self_cache[:, :, 0].reshape(seq_dev, cache_len, head_count, DK)
    cache_values = self_cache[:, :, 1].reshape(seq_dev, cache_len, head_count, DK)
    s_cache = jnp.einsum(
        "tnhd,nlhd->tnhl", query, cache_keys, preferred_element_type=jnp.float32
    ) * inv
    w_cache = jnp.where(
        cache_usable[None, :, None, :], score_weight(s_cache), jnp.zeros((), jnp.bfloat16)
    )
    s_new = jnp.einsum(
        "tnhd,unhd->tnhu", query, key_new, preferred_element_type=jnp.float32
    ) * inv
    step_at = jnp.arange(steps, dtype=jnp.int32)
    new_usable = step_at[None, :] <= step_at[:, None]
    w_new = jnp.where(
        new_usable[:, None, None, :], score_weight(s_new), jnp.zeros((), jnp.bfloat16)
    )
    weighted = jnp.einsum(
        "tnhl,nlhd->tnhd", w_cache, cache_values, preferred_element_type=jnp.float32
    ) + jnp.einsum("tnhu,unhd->tnhd", w_new, value_new, preferred_element_type=jnp.float32)
    totals = jnp.sum(w_cache.astype(jnp.float32), axis=-1) + jnp.sum(
        w_new.astype(jnp.float32), axis=-1
    )
    context = (weighted / totals[..., None]).reshape(steps, seq_dev, width).astype(jnp.bfloat16)
    context_all = rows_gather(context)
    partial_out = jnp.einsum(
        "tsw,wf->tsf", context_all, w_out_self, preferred_element_type=jnp.float32
    )
    partial_out, w_q_gained = lax.optimization_barrier((partial_out, w_q_gained))
    residual = current + tensor_sum(partial_out)

    cq = jnp.einsum(
        "tsd,dw->tsw", residual.astype(jnp.bfloat16), w_q_gained, preferred_element_type=jnp.float32
    )
    own = rows_reduce_scatter(with_sumsq(cq, residual), seq_dev)
    cross_query = split_norm(own, width).reshape(steps, seq_dev, head_count, DK)
    cross_keys = cross_kv[:, :, 0].reshape(seq_dev, source_len, head_count, DK)
    cross_values = cross_kv[:, :, 1].reshape(seq_dev, source_len, head_count, DK)
    s_cross = jnp.einsum(
        "tnhd,nlhd->tnhl", cross_query, cross_keys, preferred_element_type=jnp.float32
    ) * inv
    w_cross = jnp.where(
        cross_usable[None, :, None, :], score_weight(s_cross), jnp.zeros((), jnp.bfloat16)
    )
    weighted = jnp.einsum(
        "tnhl,nlhd->tnhd", w_cross, cross_values, preferred_element_type=jnp.float32
    )
    totals = jnp.sum(w_cross.astype(jnp.float32), axis=-1)
    context = (weighted / totals[..., None]).reshape(steps, seq_dev, width).astype(jnp.bfloat16)
    context_all = rows_gather(context)
    output_rows = residual + tensor_sum(
        jnp.einsum("tsw,wf->tsf", context_all, w_out_cross, preferred_element_type=jnp.float32)
    )
    return output_rows.astype(jnp.bfloat16)


def solution(mesh):
    in_specs = (
        P(None, "dp", "enc"),
        P(("dp", "enc"), None, None, "tensor"),
        P(("dp", "enc"), None, None, "tensor"),
        P(),
        P(),
        P(),
        P("enc"),
        P("enc", None, "tensor"),
        P("tensor", "enc"),
        P("enc"),
        P("enc", "tensor"),
        P("tensor", "enc"),
    )
    out_specs = P(None, "dp", "enc")
    return jax.shard_map(
        on_device, mesh=mesh, in_specs=in_specs, out_specs=out_specs, check_vma=False
    )
```

```python
import math

import jax
import jax.numpy as jnp
from jax import lax
from jax.sharding import PartitionSpec as P

D = 4096
DK = 256


EPSILON = 1e-06
LANE = 128


def score_weight(scores):
    return jnp.exp(scores).astype(jnp.bfloat16)


def rows_gather(chunk):
    n_enc = lax.axis_size("enc")
    steps, owned, width = chunk.shape
    send = jnp.broadcast_to(chunk[None], (n_enc, steps, owned, width))
    got = lax.all_to_all(send, "enc", 0, 0, tiled=True)
    return got.transpose(1, 0, 2, 3).reshape(steps, n_enc * owned, width)


def tensor_sum(value):
    n_t = lax.axis_size("tensor")
    value = value.astype(jnp.bfloat16)
    terms = [value] + [
        lax.ppermute(value, "tensor", [(i, i ^ k) for i in range(n_t)]) for k in range(1, n_t)
    ]
    terms = [term.astype(jnp.float32) for term in terms]
    while len(terms) > 1:
        terms = [terms[k] + terms[k + 1] for k in range(0, len(terms), 2)]
    return terms[0]


def with_sumsq(partial, rows_in):
    squares = jnp.sum(rows_in * rows_in, axis=-1, keepdims=True)
    high = squares.astype(jnp.bfloat16)
    low = jnp.where(
        jnp.isfinite(squares), squares - high.astype(jnp.float32), 0.0
    ).astype(jnp.bfloat16)
    pad = jnp.zeros(rows_in.shape[:-1] + (LANE - 2,), jnp.bfloat16)
    return jnp.concatenate([partial.astype(jnp.bfloat16), high, low, pad], axis=-1)


def rows_reduce_scatter(partial, owned):
    n_enc = lax.axis_size("enc")
    steps, rows, cols = partial.shape
    send = partial.reshape(steps, n_enc, owned, cols).transpose(1, 0, 2, 3)
    got = lax.all_to_all(send, "enc", 0, 0, tiled=True)
    return jnp.sum(got.astype(jnp.float32), axis=0)


def split_norm(packed, width):
    squares = packed[..., width] + packed[..., width + 1]
    scale = lax.rsqrt(squares / D + EPSILON)
    return (packed[..., :width] * scale[..., None]).astype(jnp.bfloat16)


def exchange_sources(src_pool, assign, my_sources, block_at, enc_at, dp_at, dp_count, enc_count, seq_dev):
    assert seq_dev == dp_count
    my_block = block_at
    source_block = my_sources // seq_dev
    source_row = my_sources % seq_dev
    received = []
    for shift in range(dp_count):
        if shift == 0:
            wanted = my_sources
        else:
            target = (dp_at + shift) % dp_count
            wanted = lax.dynamic_slice_in_dim(
                assign, (target * enc_count + enc_at) * seq_dev, seq_dev
            )
        hit = (wanted // seq_dev) == my_block
        row = jnp.sum(jnp.where(hit, wanted % seq_dev, 0))
        piece = lax.dynamic_index_in_dim(src_pool, row, axis=0, keepdims=False)
        if shift:
            piece = lax.ppermute(
                piece, "dp", [(i, (i + shift) % dp_count) for i in range(dp_count)]
            )
        received.append(piece)
    sender_block = [
        ((dp_at - shift) % dp_count) * enc_count + enc_at for shift in range(dp_count)
    ]
    cross_kv = received[0][None]
    cross_kv = jnp.broadcast_to(cross_kv, (seq_dev,) + cross_kv.shape[1:])
    for shift in range(1, dp_count):
        cross_kv = jnp.where(
            (source_block == sender_block[shift])[:, None, None, None],
            received[shift][None],
            cross_kv,
        )
    return cross_kv


def on_device(
    hidden_in,
    self_cache,
    src_pool,
    assign,
    src_len,
    positions,
    gain_self,
    w_qkv,
    w_out_self,
    gain_cross,
    w_q_cross,
    w_out_cross,
):
    dp_count = lax.axis_size("dp")
    enc_count = lax.axis_size("enc")
    seq_dev = self_cache.shape[0]
    per_pair = seq_dev // dp_count
    cache_len = self_cache.shape[1]
    source_len = src_pool.shape[1]
    width = self_cache.shape[3]
    head_count = width // DK
    steps = hidden_in.shape[0]
    enc_at = lax.axis_index("enc")
    dp_at = lax.axis_index("dp")
    block_at = dp_at * enc_count + enc_at
    slot_index = jnp.arange(seq_dev, dtype=jnp.int32)
    my_slots = block_at * seq_dev + slot_index
    my_positions = lax.dynamic_slice_in_dim(positions, block_at * seq_dev, seq_dev)
    my_sources = lax.dynamic_slice_in_dim(assign, block_at * seq_dev, seq_dev)
    place_at = jnp.arange(cache_len, dtype=jnp.int32)
    cache_usable = place_at[None, :] < my_positions[:, None]
    token_at = jnp.arange(source_len, dtype=jnp.int32)
    source_at = jnp.arange(src_len.shape[0], dtype=jnp.int32)
    my_len = jnp.sum(
        jnp.where(source_at[None, :] == my_sources[:, None], src_len[None, :], 0), axis=1
    )
    cross_usable = token_at[None, :] < my_len[:, None]

    w_q_gained = (gain_cross[:, None] * w_q_cross.astype(jnp.float32)).astype(jnp.bfloat16)

    current = hidden_in.astype(jnp.float32)
    scaled = (current * gain_self[None, None, :]).astype(jnp.bfloat16)
    proj = jnp.einsum("tsd,dcw->tscw", scaled, w_qkv, preferred_element_type=jnp.float32)
    proj = proj.reshape(steps, current.shape[1], 3 * width)
    own = rows_reduce_scatter(with_sumsq(proj, current), seq_dev)
    qkv = split_norm(own, 3 * width).reshape(steps, seq_dev, 3, head_count, DK)
    query = qkv[:, :, 0]
    key_new = qkv[:, :, 1]
    value_new = qkv[:, :, 2]

    inv = 1.0 / math.sqrt(DK)
    cache_keys = self_cache[:, :, 0].reshape(seq_dev, cache_len, head_count, DK)
    cache_values = self_cache[:, :, 1].reshape(seq_dev, cache_len, head_count, DK)
    s_cache = jnp.einsum(
        "tnhd,nlhd->tnhl", query, cache_keys, preferred_element_type=jnp.float32
    ) * inv
    w_cache = jnp.where(
        cache_usable[None, :, None, :], score_weight(s_cache), jnp.zeros((), jnp.bfloat16)
    )
    s_new = jnp.einsum(
        "tnhd,unhd->tnhu", query, key_new, preferred_element_type=jnp.float32
    ) * inv
    step_at = jnp.arange(steps, dtype=jnp.int32)
    new_usable = step_at[None, :] <= step_at[:, None]
    w_new = jnp.where(
        new_usable[:, None, None, :], score_weight(s_new), jnp.zeros((), jnp.bfloat16)
    )
    weighted = jnp.einsum(
        "tnhl,nlhd->tnhd", w_cache, cache_values, preferred_element_type=jnp.float32
    ) + jnp.einsum("tnhu,unhd->tnhd", w_new, value_new, preferred_element_type=jnp.float32)
    totals = jnp.sum(w_cache.astype(jnp.float32), axis=-1) + jnp.sum(
        w_new.astype(jnp.float32), axis=-1
    )
    context = (weighted / totals[..., None]).reshape(steps, seq_dev, width).astype(jnp.bfloat16)
    context_all = rows_gather(context)
    partial_out = jnp.einsum(
        "tsw,wf->tsf", context_all, w_out_self, preferred_element_type=jnp.float32
    )
    partial_out, src_late, w_q_gained = lax.optimization_barrier(
        (partial_out, src_pool, w_q_gained)
    )
    cross_kv = exchange_sources(
        src_late, assign, my_sources, block_at, enc_at, dp_at, dp_count, enc_count, seq_dev
    )
    residual = current + tensor_sum(partial_out)

    cq = jnp.einsum(
        "tsd,dw->tsw", residual.astype(jnp.bfloat16), w_q_gained, preferred_element_type=jnp.float32
    )
    n_enc = enc_count
    blocks = cq.reshape(steps, n_enc, seq_dev, width).transpose(1, 0, 2, 3)
    squares = jnp.sum(residual * residual, axis=-1).reshape(steps, n_enc, seq_dev)
    squares = squares.transpose(1, 0, 2).reshape(n_enc, steps * seq_dev)
    high = squares.astype(jnp.bfloat16)
    low = jnp.where(
        jnp.isfinite(squares), squares - high.astype(jnp.float32), 0.0
    ).astype(jnp.bfloat16)
    tail = jnp.concatenate(
        [high, low, jnp.zeros((n_enc, LANE - 2 * steps * seq_dev), jnp.bfloat16)], axis=-1
    )
    send = jnp.concatenate(
        [blocks.astype(jnp.bfloat16).reshape(n_enc, steps * seq_dev * width), tail], axis=-1
    )
    got = jnp.sum(lax.all_to_all(send, "enc", 0, 0, tiled=True).astype(jnp.float32), axis=0)
    body = got[: steps * seq_dev * width].reshape(steps, seq_dev, width)
    cut = steps * seq_dev * width
    sums = got[cut : cut + steps * seq_dev] + got[cut + steps * seq_dev : cut + 2 * steps * seq_dev]
    scale = lax.rsqrt(sums.reshape(steps, seq_dev) / D + EPSILON)
    cross_query = (body * scale[..., None]).astype(jnp.bfloat16).reshape(
        steps, seq_dev, head_count, DK
    )
    cross_keys = cross_kv[:, :, 0].reshape(seq_dev, source_len, head_count, DK)
    cross_values = cross_kv[:, :, 1].reshape(seq_dev, source_len, head_count, DK)
    s_cross = jnp.einsum(
        "tnhd,nlhd->tnhl", cross_query, cross_keys, preferred_element_type=jnp.float32
    ) * inv
    w_cross = jnp.where(
        cross_usable[None, :, None, :], score_weight(s_cross), jnp.zeros((), jnp.bfloat16)
    )
    weighted = jnp.einsum(
        "tnhl,nlhd->tnhd", w_cross, cross_values, preferred_element_type=jnp.float32
    )
    totals = jnp.sum(w_cross.astype(jnp.float32), axis=-1)
    context = (weighted / totals[..., None]).reshape(steps, seq_dev, width).astype(jnp.bfloat16)
    context_all = rows_gather(context)
    output_rows = residual + tensor_sum(
        jnp.einsum("tsw,wf->tsf", context_all, w_out_cross, preferred_element_type=jnp.float32)
    )
    return output_rows.astype(jnp.bfloat16)


def solution(mesh):
    in_specs = (
        P(None, "dp", "enc"),
        P(("dp", "enc"), None, None, "tensor"),
        P(("dp", "enc"), None, None, "tensor"),
        P(),
        P(),
        P(),
        P("enc"),
        P("enc", None, "tensor"),
        P("tensor", "enc"),
        P("enc"),
        P("enc", "tensor"),
        P("tensor", "enc"),
    )
    out_specs = P(None, "dp", "enc")
    return jax.shard_map(
        on_device, mesh=mesh, in_specs=in_specs, out_specs=out_specs, check_vma=False
    )
```

```python
import math

import jax
import jax.numpy as jnp
from jax import lax
from jax.sharding import PartitionSpec as P

D = 4096
DK = 256


EPSILON = 1e-06
LANE = 128


def score_weight(scores):
    return jnp.exp(scores).astype(jnp.bfloat16)


def rows_gather(chunk):
    n_enc = lax.axis_size("enc")
    steps, owned, width = chunk.shape
    send = jnp.broadcast_to(chunk[None], (n_enc, steps, owned, width))
    return lax.all_to_all(send, "enc", 0, 0, tiled=True)


def tensor_sum(value):
    n_t = lax.axis_size("tensor")
    value = value.astype(jnp.bfloat16)
    terms = [value] + [
        lax.ppermute(value, "tensor", [(i, i ^ k) for i in range(n_t)]) for k in range(1, n_t)
    ]
    terms = [term.astype(jnp.float32) for term in terms]
    while len(terms) > 1:
        terms = [terms[k] + terms[k + 1] for k in range(0, len(terms), 2)]
    return terms[0]


def with_sumsq(partial, rows_in):
    squares = jnp.sum(rows_in * rows_in, axis=-1, keepdims=True)
    high = squares.astype(jnp.bfloat16)
    low = jnp.where(
        jnp.isfinite(squares), squares - high.astype(jnp.float32), 0.0
    ).astype(jnp.bfloat16)
    pad = jnp.zeros(rows_in.shape[:-1] + (LANE - 2,), jnp.bfloat16)
    return jnp.concatenate([partial.astype(jnp.bfloat16), high, low, pad], axis=-1)


def rows_reduce_scatter(partial, owned):
    n_enc = lax.axis_size("enc")
    steps, rows, cols = partial.shape
    send = partial.reshape(steps, n_enc, owned, cols).transpose(1, 0, 2, 3)
    got = lax.all_to_all(send, "enc", 0, 0, tiled=True)
    return jnp.sum(got.astype(jnp.float32), axis=0)


def split_norm(packed, width):
    squares = packed[..., width] + packed[..., width + 1]
    scale = lax.rsqrt(squares / D + EPSILON)
    return (packed[..., :width] * scale[..., None]).astype(jnp.bfloat16)


def exchange_sources(src_pool, assign, my_sources, block_at, enc_at, dp_at, dp_count, enc_count, seq_dev):
    assert seq_dev == dp_count
    my_block = block_at
    source_block = my_sources // seq_dev
    source_row = my_sources % seq_dev
    received = []
    for shift in range(dp_count):
        if shift == 0:
            wanted = my_sources
        else:
            target = (dp_at + shift) % dp_count
            wanted = lax.dynamic_slice_in_dim(
                assign, (target * enc_count + enc_at) * seq_dev, seq_dev
            )
        hit = (wanted // seq_dev) == my_block
        row = jnp.sum(jnp.where(hit, wanted % seq_dev, 0))
        piece = lax.dynamic_index_in_dim(src_pool, row, axis=0, keepdims=False)
        if shift:
            piece = lax.ppermute(
                piece, "dp", [(i, (i + shift) % dp_count) for i in range(dp_count)]
            )
        received.append(piece)
    sender_block = [
        ((dp_at - shift) % dp_count) * enc_count + enc_at for shift in range(dp_count)
    ]
    cross_kv = received[0][None]
    cross_kv = jnp.broadcast_to(cross_kv, (seq_dev,) + cross_kv.shape[1:])
    for shift in range(1, dp_count):
        cross_kv = jnp.where(
            (source_block == sender_block[shift])[:, None, None, None],
            received[shift][None],
            cross_kv,
        )
    return cross_kv


def on_device(
    hidden_in,
    self_cache,
    src_pool,
    assign,
    src_len,
    positions,
    gain_self,
    w_qkv,
    w_out_self,
    gain_cross,
    w_q_cross,
    w_out_cross,
):
    dp_count = lax.axis_size("dp")
    enc_count = lax.axis_size("enc")
    seq_dev = self_cache.shape[0]
    per_pair = seq_dev // dp_count
    cache_len = self_cache.shape[1]
    source_len = src_pool.shape[1]
    width = self_cache.shape[3]
    head_count = width // DK
    steps = hidden_in.shape[0]
    enc_at = lax.axis_index("enc")
    dp_at = lax.axis_index("dp")
    block_at = dp_at * enc_count + enc_at
    slot_index = jnp.arange(seq_dev, dtype=jnp.int32)
    my_slots = block_at * seq_dev + slot_index
    my_positions = lax.dynamic_slice_in_dim(positions, block_at * seq_dev, seq_dev)
    my_sources = lax.dynamic_slice_in_dim(assign, block_at * seq_dev, seq_dev)
    place_at = jnp.arange(cache_len, dtype=jnp.int32)
    cache_usable = place_at[None, :] < my_positions[:, None]
    token_at = jnp.arange(source_len, dtype=jnp.int32)
    source_at = jnp.arange(src_len.shape[0], dtype=jnp.int32)
    my_len = jnp.sum(
        jnp.where(source_at[None, :] == my_sources[:, None], src_len[None, :], 0), axis=1
    )
    cross_usable = token_at[None, :] < my_len[:, None]

    w_q_gained = (gain_cross[:, None] * w_q_cross.astype(jnp.float32)).astype(jnp.bfloat16)

    current = hidden_in.astype(jnp.float32)
    scaled = (current * gain_self[None, None, :]).astype(jnp.bfloat16)
    proj = jnp.einsum("tsd,dcw->tscw", scaled, w_qkv, preferred_element_type=jnp.float32)
    proj = proj.reshape(steps, current.shape[1], 3 * width)
    own = rows_reduce_scatter(with_sumsq(proj, current), seq_dev)
    qkv = split_norm(own, 3 * width).reshape(steps, seq_dev, 3, head_count, DK)
    query = qkv[:, :, 0]
    key_new = qkv[:, :, 1]
    value_new = qkv[:, :, 2]

    inv = 1.0 / math.sqrt(DK)
    cache_keys = self_cache[:, :, 0].reshape(seq_dev, cache_len, head_count, DK)
    cache_values = self_cache[:, :, 1].reshape(seq_dev, cache_len, head_count, DK)
    s_cache = jnp.einsum(
        "tnhd,nlhd->tnhl", query, cache_keys, preferred_element_type=jnp.float32
    ) * inv
    w_cache = jnp.where(
        cache_usable[None, :, None, :], score_weight(s_cache), jnp.zeros((), jnp.bfloat16)
    )
    s_new = jnp.einsum(
        "tnhd,unhd->tnhu", query, key_new, preferred_element_type=jnp.float32
    ) * inv
    step_at = jnp.arange(steps, dtype=jnp.int32)
    new_usable = step_at[None, :] <= step_at[:, None]
    w_new = jnp.where(
        new_usable[:, None, None, :], score_weight(s_new), jnp.zeros((), jnp.bfloat16)
    )
    weighted = jnp.einsum(
        "tnhl,nlhd->tnhd", w_cache, cache_values, preferred_element_type=jnp.float32
    ) + jnp.einsum("tnhu,unhd->tnhd", w_new, value_new, preferred_element_type=jnp.float32)
    totals = jnp.sum(w_cache.astype(jnp.float32), axis=-1) + jnp.sum(
        w_new.astype(jnp.float32), axis=-1
    )
    context = (weighted / totals[..., None]).reshape(steps, seq_dev, width).astype(jnp.bfloat16)
    context_all = rows_gather(context)
    current_blocks = current.reshape(steps, enc_count, seq_dev, -1).transpose(1, 0, 2, 3)
    partial_out = jnp.einsum(
        "jtsw,wf->jtsf", context_all, w_out_self, preferred_element_type=jnp.float32
    )
    partial_out, src_late, w_q_gained = lax.optimization_barrier(
        (partial_out, src_pool, w_q_gained)
    )
    cross_kv = exchange_sources(
        src_late, assign, my_sources, block_at, enc_at, dp_at, dp_count, enc_count, seq_dev
    )
    residual = current_blocks + tensor_sum(partial_out)

    cq = jnp.einsum(
        "jtsd,dw->jtsw", residual.astype(jnp.bfloat16), w_q_gained, preferred_element_type=jnp.float32
    )
    got = lax.all_to_all(with_sumsq(cq, residual), "enc", 0, 0, tiled=True)
    own = jnp.sum(got.astype(jnp.float32), axis=0)
    cross_query = split_norm(own, width).reshape(steps, seq_dev, head_count, DK)
    cross_keys = cross_kv[:, :, 0].reshape(seq_dev, source_len, head_count, DK)
    cross_values = cross_kv[:, :, 1].reshape(seq_dev, source_len, head_count, DK)
    s_cross = jnp.einsum(
        "tnhd,nlhd->tnhl", cross_query, cross_keys, preferred_element_type=jnp.float32
    ) * inv
    w_cross = jnp.where(
        cross_usable[None, :, None, :], score_weight(s_cross), jnp.zeros((), jnp.bfloat16)
    )
    weighted = jnp.einsum(
        "tnhl,nlhd->tnhd", w_cross, cross_values, preferred_element_type=jnp.float32
    )
    totals = jnp.sum(w_cross.astype(jnp.float32), axis=-1)
    context = (weighted / totals[..., None]).reshape(steps, seq_dev, width).astype(jnp.bfloat16)
    context_all = rows_gather(context)
    output_rows = residual + tensor_sum(
        jnp.einsum("jtsw,wf->jtsf", context_all, w_out_cross, preferred_element_type=jnp.float32)
    )
    output_rows = output_rows.astype(jnp.bfloat16).transpose(1, 0, 2, 3)
    return output_rows.reshape(steps, enc_count * seq_dev, -1)


def solution(mesh):
    in_specs = (
        P(None, "dp", "enc"),
        P(("dp", "enc"), None, None, "tensor"),
        P(("dp", "enc"), None, None, "tensor"),
        P(),
        P(),
        P(),
        P("enc"),
        P("enc", None, "tensor"),
        P("tensor", "enc"),
        P("enc"),
        P("enc", "tensor"),
        P("tensor", "enc"),
    )
    out_specs = P(None, "dp", "enc")
    return jax.shard_map(
        on_device, mesh=mesh, in_specs=in_specs, out_specs=out_specs, check_vma=False
    )
```
